512 devices in a mesh: rows: 32 (over x, y_hi, core), cols: 16 (over z, y_lo).
Axes of the slice: x: 4, y: 8 (y_hi: 4, y_lo: 2; y = y_hi * 2 + y_lo), z: 8, core: 2. Of those that a mesh axis runs over, the one named last changes fastest.
Arguments:
- greens: bfloat16 [512, 262144], P('cols', 'rows'), may hold values from -0.5 to 0.5
- slip_values: bfloat16 [8192, 128], P('cols'), may hold values from 0.5 to 4
- rupture_ids: int32 [8192, 128], P('cols'), may hold values from -1 to 511, as said below
- win_point: int32 [4096], P('rows'), may hold values from 0 to 1023, never falling along the last dimension, each value on 1 to 32 neighbouring positions
Outputs:
- window_peak: float32 [8192, 4096], P('cols', 'rows')
The draws below stay inside these ranges and needn't reach their ends.
Inputs may be any that keep to these rules, and one draw needn't show every extreme that they name: `rupture_ids`: each row lists its sources as one run of consecutive source numbers in its first slots and -1 in the rest; some row fills all 128 slots. `win_point`: never falls along the windows; every point holds 1 to 32 consecutive windows and some point exactly 32.
All inputs are finite; a program needn't handle non-finite values.
Results may differ from the reference program's by a relative error of at most 0.0003.
Values may be sent and summed in bfloat16 or wider, within the bound.
No kernel may reach another device: no remote copies, remote signals or barrier semaphores. Data moves between devices by JAX's collectives and lax.ppermute only.
A program may use at most 64 MiB of HBM per device.

```python
import math
import jax
import jax.numpy as jnp
import numpy as np
from jax import lax

S = 512
LMAX = 128
TSTEP = 64
MOST = 32
WIN_DEV = 128
ROWS_DEV = 8192
ROWS = 262144
NWIN = 4096
POINTS = 1024
K = 8192


def draw_rupture_ids(key, part):
    first_key, second_key = jax.random.split(key)
    lengths = jax.random.randint(first_key, (K,), 1, LMAX + 1)
    lengths = lengths.at[0].set(LMAX)
    starts = jax.random.randint(second_key, (K,), 0, S - lengths + 1)
    slots = jnp.arange(LMAX, dtype=jnp.int32)[None, :]
    return jnp.where(slots < lengths[:, None], starts[:, None] + slots, -1).astype(jnp.int32)


def shard_levels(own_key, dims, cuts, smallest, high):
    loudness, own = 1.0, jax.random.fold_in(own_key, 6)
    for position, parts in cuts:
        heights = jnp.exp(jax.random.uniform(jax.random.fold_in(own, position), (parts,), jnp.float32, smallest / len(cuts), high / len(cuts)))
        loudness = loudness * jnp.repeat(heights, dims[position] // parts).reshape([-1 if axis == position else 1 for axis in range(len(dims))])
    return loudness


def split_up(number_of, total, reach, lean):
    portions = [(1 << 20) // math.isqrt(rank ** lean) + 1 for rank in range(2, number_of + 1)]
    spare, holding = total - reach - (number_of - 1), [1] * (number_of - 1)
    while spare > 0:
        candidates = [i for i in range(number_of - 1) if holding[i] < reach]
        mass, remaining = sum([portions[i] for i in candidates]), spare
        for i in candidates:
            extra = min(reach - holding[i], max(1, remaining * portions[i] // mass), spare)
            holding[i] = holding[i] + extra
            spare = spare - extra
    return np.array([reach] + holding)


def ragged(key, count, total, reach, slope):
    if count == 2:
        one = jax.random.randint(key, (), max(1, total - reach), min(reach, total - 1) + 1)
        return jnp.stack([one, total - one])
    sizes = jnp.asarray(split_up(count, total, reach, slope), jnp.int32)
    couples = (count - 1) // 2
    donor, sink = sizes[1:1 + 2 * couples:2], sizes[2:2 + 2 * couples:2]
    slack = jnp.minimum(donor - 1, reach - sink)
    passed = jax.random.randint(jax.random.fold_in(key, 1), (couples,), 0, 1 << 20) % (slack + 1)
    sizes = sizes.at[1:1 + 2 * couples:2].set(donor - passed).at[2:2 + 2 * couples:2].set(sink + passed)
    return sizes[jax.random.permutation(jax.random.fold_in(key, 2), count)]


def gaussian(own_key, extent, spread, bound, cuts=(), kind=jnp.bfloat16):
    drawn = jax.random.normal(own_key, extent, jnp.float32) * spread
    if len(cuts) > 0:
        drawn = shard_levels(own_key, extent, cuts, -0.22, 0.18) * drawn
    return jnp.clip(drawn, min=-bound, max=bound).astype(kind)


def setup_inputs(seed: int = 0) -> dict:
    streams_of = jax.random.split(jax.random.key(seed), 5)
    greens = gaussian(streams_of[0], (S, ROWS), LMAX ** -0.5, 0.5, ((0, 16), (1, 32)))
    slip_values = jnp.clip(jnp.exp(math.log(4.0) - 2.0794415 * jax.random.uniform(streams_of[1], (K, LMAX), jnp.float32) ** shard_levels(streams_of[1], (K, LMAX), ((0, 16),), -0.2, 0.2)), 0.5, 4.0).astype(jnp.bfloat16)
    rupture_ids = draw_rupture_ids(jax.random.fold_in(streams_of[4], 71), 0)
    win_point = jnp.searchsorted(jnp.cumsum(ragged(streams_of[3], POINTS, NWIN, MOST, 0)), jnp.arange(NWIN), side="right").astype(jnp.int32)
    return dict(greens=greens, slip_values=slip_values, rupture_ids=rupture_ids, win_point=win_point)


def dense_slips(slip_values, rupture_ids, count, width):
    target = jnp.where(rupture_ids < 0, width, rupture_ids).astype(jnp.int32)
    scen_index = jnp.broadcast_to(jnp.arange(count, dtype=jnp.int32)[:, None], rupture_ids.shape)
    table = jnp.zeros((count, width), jnp.float32).at[scen_index, target].add(slip_values.astype(jnp.float32), mode="drop")
    return table.astype(jnp.bfloat16)


def reference(greens, slip_values, rupture_ids, win_point):
    dense = dense_slips(slip_values, rupture_ids, K, S)
    blocks = ROWS // ROWS_DEV

    def one_block(block_index):
        panel = lax.dynamic_slice_in_dim(greens, block_index * ROWS_DEV, ROWS_DEV, 1)
        wave = jnp.dot(dense, panel, preferred_element_type=jnp.float32)
        return jnp.max(wave.reshape(K, WIN_DEV, TSTEP), axis=2)

    per_block = lax.map(one_block, jnp.arange(blocks, dtype=jnp.int32))
    window_max = jnp.transpose(per_block, (1, 0, 2)).reshape(K, NWIN)
    point_max = jax.ops.segment_max(window_max.T, win_point, num_segments=POINTS)
    return point_max[win_point].T
```

```python
import jax
import jax.numpy as jnp
from jax import lax
from jax.sharding import Mesh
from jax.sharding import PartitionSpec as P

TSTEP = 64
COLS = ("cols_0", "cols_1")
SPLIT = "cols_0"
SHARE = "cols_1"


def extended(cells, sides, width):
    for axis, dim in sides:
        count = lax.axis_size(axis)
        ends = count - 1
        head = lax.slice_in_dim(cells, 0, width, axis=dim)
        tail = lax.slice_in_dim(cells, cells.shape[dim] - width, cells.shape[dim], axis=dim)
        cells = jnp.concatenate(
            [
                lax.ppermute(tail, axis, [(i, (i + 1) % count) for i in range(ends)]),
                cells,
                lax.ppermute(head, axis, [((i + 1) % count, i) for i in range(ends)]),
            ],
            axis=dim,
        )
    return cells


def shifted_slips(values, starts, width):
    count, slots = values.shape
    dense = jnp.concatenate([values, jnp.zeros((count, width - slots), values.dtype)], axis=1)
    bits = max(1, (width - 1).bit_length())
    for bit in range(bits):
        step = 1 << bit
        rolled = jnp.concatenate([dense[:, width - step:], dense[:, : width - step]], axis=1)
        dense = jnp.where(((starts >> bit) & 1)[:, None] == 1, rolled, dense)
    return dense


def combine(earlier, later):
    flag = jnp.logical_or(earlier[0], later[0])
    value = jnp.where(later[0], later[1], jnp.maximum(earlier[1], later[1]))
    return (flag, value)


def point_peaks(window_max, win_point):
    windows = window_max.shape[1]
    begins = jnp.concatenate([jnp.ones((1,), bool), win_point[1:] != win_point[:-1]])
    finals = jnp.concatenate([win_point[:-1] != win_point[1:], jnp.ones((1,), bool)])
    begin_flags = jnp.broadcast_to(begins[None, :], window_max.shape)
    final_flags = jnp.broadcast_to(finals[None, :], window_max.shape)
    forward = lax.associative_scan(combine, (begin_flags, window_max), axis=1)[1]
    backward = lax.associative_scan(combine, (final_flags, window_max), reverse=True, axis=1)[1]
    local_peak = jnp.maximum(forward, backward)
    edge_values = jnp.stack([backward[:, 0], forward[:, windows - 1]], axis=1)
    edge_points = jnp.stack([win_point[0] + 1, win_point[windows - 1] + 1]).astype(jnp.float32)[
        None, :
    ]
    padded_values, padded_points = (
        extended(edge_values, (("rows", 1),), 1),
        extended(edge_points, (("rows", 1),), 1),
    )
    point_code = (win_point + 1).astype(jnp.float32)[None, :]
    from_left = jnp.maximum(local_peak, padded_values[:, 0:1])
    local_peak = jnp.where(point_code == padded_points[0, 0], from_left, local_peak)
    from_right = jnp.maximum(local_peak, padded_values[:, 3:4])
    local_peak = jnp.where(point_code == padded_points[0, 3], from_right, local_peak)
    return local_peak


def local(greens, slip_values, rupture_ids, win_point):
    parts = lax.axis_size(SPLIT)
    shares = lax.axis_size(SHARE)
    own_sources, rows = greens.shape
    width = own_sources * parts * shares
    scen = slip_values.shape[0]
    block = rows // parts

    listed = rupture_ids >= 0
    values = jnp.where(listed, slip_values, jnp.zeros_like(slip_values))
    starts = jnp.maximum(rupture_ids[:, 0], 0)
    all_values = lax.all_gather(values, SPLIT, axis=0, tiled=True)
    all_starts = lax.all_gather(starts, SPLIT, axis=0, tiled=True)

    pieces = greens.reshape(own_sources, parts, block)
    pieces = lax.all_to_all(pieces, SPLIT, 1, 0, tiled=True)
    pieces = pieces.reshape(parts, own_sources, block)
    pieces = lax.all_gather(pieces, SHARE, axis=0, tiled=False)
    panel_t = jnp.transpose(pieces, (3, 1, 0, 2)).reshape(block, width)

    dense = shifted_slips(all_values, all_starts, width)
    wave_t = lax.dot_general(
        panel_t, dense, (((1,), (1,)), ((), ())), preferred_element_type=jnp.float32
    )
    win_block = block // TSTEP
    maxima = jnp.max(wave_t.reshape(win_block, TSTEP, parts * scen), axis=1)
    maxima = maxima.reshape(win_block, parts, scen)
    maxima = lax.all_to_all(maxima, SPLIT, 1, 0, tiled=True)
    window_max = maxima.reshape(parts * win_block, scen).T
    return point_peaks(window_max, win_point)


def solution(mesh):
    split = Mesh(mesh.devices.reshape(mesh.shape["rows"], 8, 2), ("rows", "cols_0", "cols_1"))
    in_specs = (P(COLS, "rows"), P(COLS, None), P(COLS, None), P("rows"))
    out_specs = P(COLS, "rows")
    return jax.shard_map(local, mesh=split, in_specs=in_specs, out_specs=out_specs, check_vma=False)
```

```python
import jax
import jax.numpy as jnp
from jax import lax
from jax.experimental import pallas as pl
from jax.experimental.pallas import tpu as pltpu
from jax.sharding import Mesh
from jax.sharding import PartitionSpec as P

TSTEP = 64
COLS = ("cols_0", "cols_1")
SPLIT = "cols_0"
SHARE = "cols_1"
CODE = 32


def extended(cells, sides, width):
    for axis, dim in sides:
        count = lax.axis_size(axis)
        ends = count - 1
        head = lax.slice_in_dim(cells, 0, width, axis=dim)
        tail = lax.slice_in_dim(cells, cells.shape[dim] - width, cells.shape[dim], axis=dim)
        cells = jnp.concatenate(
            [
                lax.ppermute(tail, axis, [(i, (i + 1) % count) for i in range(ends)]),
                cells,
                lax.ppermute(head, axis, [((i + 1) % count, i) for i in range(ends)]),
            ],
            axis=dim,
        )
    return cells


def wave_kernel(gt_ref, a_ref, o_ref):
    slots = a_ref.shape[0] - 16
    width = gt_ref.shape[1]
    lanes = a_ref.shape[1]
    code = a_ref[slots:slots + 16, :].astype(jnp.float32)
    start = (code[0:1] * CODE + code[1:2]).astype(jnp.int32)
    dense = jnp.concatenate(
        [a_ref[0:slots, :].astype(jnp.float32), jnp.zeros((width - slots, lanes), jnp.float32)], axis=0
    )
    for bit in range(max(1, (width - 1).bit_length())):
        rolled = pltpu.roll(dense, 1 << bit, 0)
        dense = jnp.where(((start >> bit) & 1) == 1, rolled, dense)
    wave = jnp.dot(gt_ref[...], dense.astype(jnp.bfloat16), preferred_element_type=jnp.float32)
    rows = wave.shape[0]
    o_ref[...] = jnp.max(wave.reshape(rows // TSTEP, TSTEP, lanes), axis=1)


def wave_maxima(panel_t, coded):
    parts, height, lanes = coded.shape
    rows, width = panel_t.shape
    return pl.pallas_call(
        wave_kernel,
        grid=(parts,),
        in_specs=[
            pl.BlockSpec((rows, width), lambda p: (0, 0)),
            pl.BlockSpec((None, height, lanes), lambda p: (p, 0, 0)),
        ],
        out_specs=pl.BlockSpec((None, rows // TSTEP, lanes), lambda p: (p, 0, 0)),
        out_shape=jax.ShapeDtypeStruct((parts, rows // TSTEP, lanes), jnp.float32),
    )(panel_t, coded)


def combine(earlier, later):
    flag = jnp.logical_or(earlier[0], later[0])
    value = jnp.where(later[0], later[1], jnp.maximum(earlier[1], later[1]))
    return (flag, value)


def point_peaks(window_max, win_point):
    windows = window_max.shape[1]
    begins = jnp.concatenate([jnp.ones((1,), bool), win_point[1:] != win_point[:-1]])
    finals = jnp.concatenate([win_point[:-1] != win_point[1:], jnp.ones((1,), bool)])
    begin_flags = jnp.broadcast_to(begins[None, :], window_max.shape)
    final_flags = jnp.broadcast_to(finals[None, :], window_max.shape)
    forward = lax.associative_scan(combine, (begin_flags, window_max), axis=1)[1]
    backward = lax.associative_scan(combine, (final_flags, window_max), reverse=True, axis=1)[1]
    local_peak = jnp.maximum(forward, backward)
    edge_values = jnp.stack([backward[:, 0], forward[:, windows - 1]], axis=1)
    edge_points = jnp.stack([win_point[0] + 1, win_point[windows - 1] + 1]).astype(jnp.float32)[
        None, :
    ]
    padded_values, padded_points = (
        extended(edge_values, (("rows", 1),), 1),
        extended(edge_points, (("rows", 1),), 1),
    )
    point_code = (win_point + 1).astype(jnp.float32)[None, :]
    from_left = jnp.maximum(local_peak, padded_values[:, 0:1])
    local_peak = jnp.where(point_code == padded_points[0, 0], from_left, local_peak)
    from_right = jnp.maximum(local_peak, padded_values[:, 3:4])
    local_peak = jnp.where(point_code == padded_points[0, 3], from_right, local_peak)
    return local_peak


def local(greens, slip_values, rupture_ids, win_point):
    parts = lax.axis_size(SPLIT)
    shares = lax.axis_size(SHARE)
    own_sources, rows = greens.shape
    width = own_sources * parts * shares
    scen = slip_values.shape[0]
    block = rows // parts

    listed = rupture_ids >= 0
    values = jnp.where(listed, slip_values, jnp.zeros_like(slip_values))
    starts = jnp.maximum(rupture_ids[:, 0], 0)
    code = jnp.stack([starts // CODE, starts % CODE]).astype(jnp.bfloat16)
    coded = jnp.concatenate([values.T, code, jnp.zeros((14, scen), jnp.bfloat16)], axis=0)
    coded = lax.all_gather(coded, SPLIT, axis=0, tiled=False)

    pieces = greens.reshape(own_sources, parts, block)
    pieces = lax.all_to_all(pieces, SPLIT, 1, 0, tiled=True)
    pieces = pieces.reshape(parts, own_sources, block)
    pieces = lax.all_gather(pieces, SHARE, axis=0, tiled=False)
    panel_t = jnp.transpose(pieces, (3, 1, 0, 2)).reshape(block, width)

    maxima = wave_maxima(panel_t, coded)
    maxima = lax.all_to_all(maxima, SPLIT, 0, 0, tiled=True)
    window_max = maxima.reshape(-1, scen).T
    return point_peaks(window_max, win_point)


def solution(mesh):
    split = Mesh(mesh.devices.reshape(mesh.shape["rows"], 8, 2), ("rows", "cols_0", "cols_1"))
    in_specs = (P(COLS, "rows"), P(COLS, None), P(COLS, None), P("rows"))
    out_specs = P(COLS, "rows")
    return jax.shard_map(local, mesh=split, in_specs=in_specs, out_specs=out_specs, check_vma=False)
```

```python
import jax
import jax.numpy as jnp
from jax import lax
from jax.experimental import pallas as pl
from jax.experimental.pallas import tpu as pltpu
from jax.sharding import Mesh
from jax.sharding import PartitionSpec as P

TSTEP = 64
COLS = ("cols_0", "cols_1")
SPLIT = "cols_0"
SHARE = "cols_1"
CODE = 32
MOST = 32


def wave_kernel(offset_ref, gt_ref, a_ref, o_ref):
    slots = a_ref.shape[0] - 16
    width = gt_ref.shape[1]
    lanes = a_ref.shape[1]
    code = a_ref[slots:slots + 16, :].astype(jnp.float32)
    start = (code[0:1] * CODE + code[1:2]).astype(jnp.int32)
    start = (start - offset_ref[0]) & (width - 1)
    dense = jnp.concatenate(
        [a_ref[0:slots, :].astype(jnp.float32), jnp.zeros((width - slots, lanes), jnp.float32)], axis=0
    )
    for bit in range(max(1, (width - 1).bit_length())):
        rolled = pltpu.roll(dense, 1 << bit, 0)
        dense = jnp.where(((start >> bit) & 1) == 1, rolled, dense)
    wave = jnp.dot(gt_ref[...], dense.astype(jnp.bfloat16), preferred_element_type=jnp.float32)
    rows = wave.shape[0]
    o_ref[...] = jnp.max(wave.reshape(rows // TSTEP, TSTEP, lanes), axis=1)


def wave_maxima(offset, panel_t, coded):
    parts, height, lanes = coded.shape
    rows, width = panel_t.shape
    assert width & (width - 1) == 0
    grid_spec = pltpu.PrefetchScalarGridSpec(
        num_scalar_prefetch=1,
        grid=(parts,),
        in_specs=[
            pl.BlockSpec((rows, width), lambda p, o: (0, 0)),
            pl.BlockSpec((None, height, lanes), lambda p, o: (p, 0, 0)),
        ],
        out_specs=pl.BlockSpec((None, rows // TSTEP, lanes), lambda p, o: (p, 0, 0)),
    )
    return pl.pallas_call(
        wave_kernel,
        grid_spec=grid_spec,
        out_shape=jax.ShapeDtypeStruct((parts, rows // TSTEP, lanes), jnp.float32),
    )(offset, panel_t, coded)


def shifted(values, step, fill):
    pad = jnp.full((abs(step),) + values.shape[1:], fill, values.dtype)
    if step > 0:
        return jnp.concatenate([pad, values[:-step]], axis=0)
    return jnp.concatenate([values[-step:], pad], axis=0)


def run_max(values, codes, reach, sign):
    step = 1
    while step < reach:
        other = shifted(values, sign * step, -jnp.inf)
        same = shifted(codes, sign * step, 0.0) == codes
        values = jnp.where(same, jnp.maximum(values, other), values)
        step *= 2
    return values


def point_peaks(window_max_t, win_point, reach):
    windows, scen = window_max_t.shape
    codes = (win_point + 1).astype(jnp.float32)[:, None]
    forward = run_max(window_max_t, codes, reach, 1)
    backward = run_max(window_max_t, codes, reach, -1)
    peak = jnp.maximum(forward, backward)
    count = lax.axis_size("rows")
    to_right = jnp.concatenate([forward[windows - 1:], jnp.broadcast_to(codes[windows - 1:], (1, scen))], axis=0)
    to_left = jnp.concatenate([backward[:1], jnp.broadcast_to(codes[:1], (1, scen))], axis=0)
    from_left = lax.ppermute(to_right, "rows", [(i, i + 1) for i in range(count - 1)])
    from_right = lax.ppermute(to_left, "rows", [(i + 1, i) for i in range(count - 1)])
    peak = jnp.where(codes == from_left[1:2], jnp.maximum(peak, from_left[0:1]), peak)
    peak = jnp.where(codes == from_right[1:2], jnp.maximum(peak, from_right[0:1]), peak)
    return peak.T


def local(greens, slip_values, rupture_ids, win_point):
    parts = lax.axis_size(SPLIT)
    shares = lax.axis_size(SHARE)
    own_sources, rows = greens.shape
    width = own_sources * parts * shares
    scen = slip_values.shape[0]
    block = rows // parts

    listed = rupture_ids >= 0
    values = jnp.where(listed, slip_values, jnp.zeros_like(slip_values))
    starts = jnp.maximum(rupture_ids[:, 0], 0)
    code = jnp.stack([starts // CODE, starts % CODE]).astype(jnp.bfloat16)
    coded = jnp.concatenate([values.T, code, jnp.zeros((14, scen), jnp.bfloat16)], axis=0)
    coded = lax.all_gather(coded, SPLIT, axis=0, tiled=False)

    count = parts * shares
    here = lax.axis_index(COLS)
    pieces = greens.reshape(own_sources, parts, block)
    received = []
    for distance in range(count):
        target = lax.rem(here + distance, count) // shares
        piece = lax.dynamic_index_in_dim(pieces, target, axis=1, keepdims=False)
        if distance > 0:
            piece = lax.ppermute(piece, COLS, [(i, (i + distance) % count) for i in range(count)])
        received.append(piece)
    ordered = [received[(count - u) % count] for u in range(count)]
    panel_t = jnp.stack(ordered).reshape(width, block).T
    offset = (here * own_sources).astype(jnp.int32).reshape(1)

    maxima = wave_maxima(offset, panel_t, coded)
    maxima = lax.all_to_all(maxima, SPLIT, 0, 0, tiled=True)
    return point_peaks(maxima.reshape(-1, scen), win_point, MOST)


def solution(mesh):
    split = Mesh(mesh.devices.reshape(mesh.shape["rows"], 8, 2), ("rows", "cols_0", "cols_1"))
    in_specs = (P(COLS, "rows"), P(COLS, None), P(COLS, None), P("rows"))
    out_specs = P(COLS, "rows")
    return jax.shard_map(local, mesh=split, in_specs=in_specs, out_specs=out_specs, check_vma=False)
```

```python
import jax
import jax.numpy as jnp
from jax import lax
from jax.experimental import pallas as pl
from jax.experimental.pallas import tpu as pltpu
from jax.sharding import Mesh
from jax.sharding import PartitionSpec as P

TSTEP = 64
COLS = ("cols_0", "cols_1")
SPLIT = "cols_0"
SHARE = "cols_1"
CODE = 32
MOST = 32


def wave_kernel(offset_ref, gt_ref, a_ref, o_ref):
    slots = a_ref.shape[0] - 16
    width = gt_ref.shape[1]
    lanes = a_ref.shape[1]
    code = a_ref[slots:slots + 16, :].astype(jnp.float32)
    start = (code[0:1] * CODE + code[1:2]).astype(jnp.int32)
    start = (start - offset_ref[0]) & (width - 1)
    dense = jnp.concatenate(
        [a_ref[0:slots, :].astype(jnp.float32), jnp.zeros((width - slots, lanes), jnp.float32)], axis=0
    )
    for bit in range(max(1, (width - 1).bit_length())):
        rolled = pltpu.roll(dense, 1 << bit, 0)
        dense = jnp.where(((start >> bit) & 1) == 1, rolled, dense)
    wave = jnp.dot(gt_ref[...], dense.astype(jnp.bfloat16), preferred_element_type=jnp.float32)
    rows = wave.shape[0]
    o_ref[...] = jnp.max(wave.reshape(rows // TSTEP, TSTEP, lanes), axis=1)


def wave_maxima(offset, panel_t, coded):
    parts, height, lanes = coded.shape
    rows, width = panel_t.shape
    assert width & (width - 1) == 0
    grid_spec = pltpu.PrefetchScalarGridSpec(
        num_scalar_prefetch=1,
        grid=(parts,),
        in_specs=[
            pl.BlockSpec((rows, width), lambda p, o: (0, 0)),
            pl.BlockSpec((None, height, lanes), lambda p, o: (p, 0, 0)),
        ],
        out_specs=pl.BlockSpec((None, rows // TSTEP, lanes), lambda p, o: (p, 0, 0)),
    )
    return pl.pallas_call(
        wave_kernel,
        grid_spec=grid_spec,
        out_shape=jax.ShapeDtypeStruct((parts, rows // TSTEP, lanes), jnp.float32),
    )(offset, panel_t, coded)


def shifted(values, step, fill):
    pad = jnp.full((abs(step),) + values.shape[1:], fill, values.dtype)
    if step > 0:
        return jnp.concatenate([pad, values[:-step]], axis=0)
    return jnp.concatenate([values[-step:], pad], axis=0)


def run_max(values, codes, reach, sign):
    step = 1
    while step < reach:
        other = shifted(values, sign * step, -jnp.inf)
        same = shifted(codes, sign * step, 0.0) == codes
        values = jnp.where(same, jnp.maximum(values, other), values)
        step *= 2
    return values


def point_peaks(window_max_t, win_point, reach):
    windows, scen = window_max_t.shape
    codes = (win_point + 1).astype(jnp.float32)[:, None]
    forward = run_max(window_max_t, codes, reach, 1)
    backward = run_max(window_max_t, codes, reach, -1)
    peak = jnp.maximum(forward, backward)
    count = lax.axis_size("rows")
    to_right = jnp.concatenate([forward[windows - 1:], jnp.broadcast_to(codes[windows - 1:], (1, scen))], axis=0)
    to_left = jnp.concatenate([backward[:1], jnp.broadcast_to(codes[:1], (1, scen))], axis=0)
    from_left = lax.ppermute(to_right, "rows", [(i, i + 1) for i in range(count - 1)])
    from_right = lax.ppermute(to_left, "rows", [(i + 1, i) for i in range(count - 1)])
    peak = jnp.where(codes == from_left[1:2], jnp.maximum(peak, from_left[0:1]), peak)
    peak = jnp.where(codes == from_right[1:2], jnp.maximum(peak, from_right[0:1]), peak)
    return peak.T


def local(greens, slip_values, rupture_ids, win_point):
    parts = lax.axis_size(SPLIT)
    shares = lax.axis_size(SHARE)
    own_sources, rows = greens.shape
    width = own_sources * parts * shares
    scen = slip_values.shape[0]
    block = rows // parts

    listed = rupture_ids >= 0
    values = jnp.where(listed, slip_values, jnp.zeros_like(slip_values))
    starts = jnp.maximum(rupture_ids[:, 0], 0)
    code = jnp.stack([starts // CODE, starts % CODE]).astype(jnp.bfloat16)
    coded = jnp.concatenate([values.T, code, jnp.zeros((14, scen), jnp.bfloat16)], axis=0)
    core = lax.rem(lax.axis_index("rows"), 2)
    half = scen // 2
    mine = lax.dynamic_slice_in_dim(coded, core * half, half, axis=1)
    mine = lax.all_gather(mine, SPLIT, axis=0, tiled=False)
    count_rows = lax.axis_size("rows")
    theirs = lax.ppermute(mine, "rows", [(i, i ^ 1) for i in range(count_rows)])
    coded = jnp.where(core == 0, jnp.concatenate([mine, theirs], axis=2), jnp.concatenate([theirs, mine], axis=2))

    pieces = greens.reshape(own_sources, parts, 1, block)
    pieces = jnp.broadcast_to(pieces, (own_sources, parts, shares, block)).reshape(own_sources, parts * shares, block)
    pieces = lax.all_to_all(pieces, COLS, 1, 0, tiled=True)
    panel_t = pieces.reshape(width, block).T
    offset = jnp.zeros((1,), jnp.int32)

    maxima = wave_maxima(offset, panel_t, coded)
    maxima = lax.all_to_all(maxima, SPLIT, 0, 0, tiled=True)
    return point_peaks(maxima.reshape(-1, scen), win_point, MOST)


def solution(mesh):
    split = Mesh(mesh.devices.reshape(mesh.shape["rows"], 8, 2), ("rows", "cols_0", "cols_1"))
    in_specs = (P(COLS, "rows"), P(COLS, None), P(COLS, None), P("rows"))
    out_specs = P(COLS, "rows")
    return jax.shard_map(local, mesh=split, in_specs=in_specs, out_specs=out_specs, check_vma=False)
```

```python
import jax
import jax.numpy as jnp
from jax import lax
from jax.experimental import pallas as pl
from jax.experimental.pallas import tpu as pltpu
from jax.sharding import Mesh
from jax.sharding import PartitionSpec as P

TSTEP = 64
COLS = ("cols_0", "cols_1")
SPLIT = "cols_0"
SHARE = "cols_1"
CODE = 32
MOST = 32
HALVES = 2


def wave_kernel(gt_ref, a_ref, o_ref):
    slots = a_ref.shape[0] - 16
    width = gt_ref.shape[1]
    lanes = a_ref.shape[1]
    code = a_ref[slots:slots + 16, :].astype(jnp.float32)
    start = (code[0:1] * CODE + code[1:2]).astype(jnp.int32)
    dense = a_ref[0:slots, :].astype(jnp.float32)
    reach = slots
    for bit in range(max(1, (width - 1).bit_length())):
        step = 1 << bit
        reach = reach + step
        extent = min(width, -(-reach // 8) * 8)
        if extent > dense.shape[0]:
            dense = jnp.concatenate([dense, jnp.zeros((extent - dense.shape[0], lanes), jnp.float32)], axis=0)
        rolled = pltpu.roll(dense, step, 0)
        dense = jnp.where(((start >> bit) & 1) == 1, rolled, dense)
    if dense.shape[0] < width:
        dense = jnp.concatenate([dense, jnp.zeros((width - dense.shape[0], lanes), jnp.float32)], axis=0)
    wave = jnp.dot(gt_ref[...], dense.astype(jnp.bfloat16), preferred_element_type=jnp.float32)
    rows = wave.shape[0]
    o_ref[...] = jnp.max(wave.reshape(rows // TSTEP, TSTEP, lanes), axis=1)


def wave_maxima(panel_t, coded):
    parts, height, lanes = coded.shape
    rows, width = panel_t.shape
    return pl.pallas_call(
        wave_kernel,
        grid=(parts,),
        in_specs=[
            pl.BlockSpec((rows, width), lambda p: (0, 0)),
            pl.BlockSpec((None, height, lanes), lambda p: (p, 0, 0)),
        ],
        out_specs=pl.BlockSpec((None, rows // TSTEP, lanes), lambda p: (p, 0, 0)),
        out_shape=jax.ShapeDtypeStruct((parts, rows // TSTEP, lanes), jnp.float32),
    )(panel_t, coded)


def shifted(values, step, fill):
    pad = jnp.full((abs(step),) + values.shape[1:], fill, values.dtype)
    if step > 0:
        return jnp.concatenate([pad, values[:-step]], axis=0)
    return jnp.concatenate([values[-step:], pad], axis=0)


def run_max(values, codes, reach, sign):
    step = 1
    while step < reach:
        other = shifted(values, sign * step, -jnp.inf)
        same = shifted(codes, sign * step, 0.0) == codes
        values = jnp.where(same, jnp.maximum(values, other), values)
        step *= 2
    return values


def point_peaks(window_max_t, win_point, reach):
    windows, scen = window_max_t.shape
    codes = (win_point + 1).astype(jnp.float32)[:, None]
    forward = run_max(window_max_t, codes, reach, 1)
    backward = run_max(window_max_t, codes, reach, -1)
    peak = jnp.maximum(forward, backward)
    count = lax.axis_size("rows")
    to_right = jnp.concatenate([forward[windows - 1:], jnp.broadcast_to(codes[windows - 1:], (1, scen))], axis=0)
    to_left = jnp.concatenate([backward[:1], jnp.broadcast_to(codes[:1], (1, scen))], axis=0)
    from_left = lax.ppermute(to_right, "rows", [(i, i + 1) for i in range(count - 1)])
    from_right = lax.ppermute(to_left, "rows", [(i + 1, i) for i in range(count - 1)])
    peak = jnp.where(codes == from_left[1:2], jnp.maximum(peak, from_left[0:1]), peak)
    peak = jnp.where(codes == from_right[1:2], jnp.maximum(peak, from_right[0:1]), peak)
    return peak.T


def local(greens, slip_values, rupture_ids, win_point):
    parts = lax.axis_size(SPLIT)
    shares = lax.axis_size(SHARE)
    own_sources, rows = greens.shape
    width = own_sources * parts * shares
    scen = slip_values.shape[0]
    block = rows // parts

    listed = rupture_ids >= 0
    values = jnp.where(listed, slip_values, jnp.zeros_like(slip_values))
    starts = jnp.maximum(rupture_ids[:, 0], 0)
    code = jnp.stack([starts // CODE, starts % CODE]).astype(jnp.bfloat16)
    coded = jnp.concatenate([values.T, code, jnp.zeros((14, scen), jnp.bfloat16)], axis=0)
    core = lax.rem(lax.axis_index("rows"), 2)
    half = scen // 2
    mine = lax.dynamic_slice_in_dim(coded, core * half, half, axis=1)
    mine = lax.all_gather(mine, SPLIT, axis=0, tiled=False)
    count_rows = lax.axis_size("rows")
    theirs = lax.ppermute(mine, "rows", [(i, i ^ 1) for i in range(count_rows)])
    coded = jnp.where(core == 0, jnp.concatenate([mine, theirs], axis=2), jnp.concatenate([theirs, mine], axis=2))

    pieces = greens.reshape(own_sources, parts, 1, block)
    pieces = jnp.broadcast_to(pieces, (own_sources, parts, shares, block)).reshape(own_sources, parts * shares, block)
    piece = block // HALVES
    outs = []
    for half in range(HALVES):
        sub = pieces[:, :, half * piece:(half + 1) * piece]
        sub = lax.all_to_all(sub, COLS, 1, 0, tiled=True)
        panel_t = sub.reshape(width, piece).T
        maxima = wave_maxima(panel_t, coded)
        outs.append(lax.all_to_all(maxima, SPLIT, 0, 0, tiled=True))
    maxima = jnp.concatenate(outs, axis=1)
    return point_peaks(maxima.reshape(-1, scen), win_point, MOST)


def solution(mesh):
    split = Mesh(mesh.devices.reshape(mesh.shape["rows"], 8, 2), ("rows", "cols_0", "cols_1"))
    in_specs = (P(COLS, "rows"), P(COLS, None), P(COLS, None), P("rows"))
    out_specs = P(COLS, "rows")
    return jax.shard_map(local, mesh=split, in_specs=in_specs, out_specs=out_specs, check_vma=False)
```

```python
import jax
import jax.numpy as jnp
from jax import lax
from jax.experimental import pallas as pl
from jax.experimental.pallas import tpu as pltpu
from jax.sharding import Mesh
from jax.sharding import PartitionSpec as P

TSTEP = 64
COLS = ("cols_0", "cols_1")
SPLIT = "cols_0"
SHARE = "cols_1"
CODE = 32
MOST = 32


def wave_kernel(gt_ref, a_ref, o_ref):
    slots = a_ref.shape[0] - 16
    width = gt_ref.shape[1]
    lanes = a_ref.shape[1]
    code = a_ref[slots:slots + 16, :].astype(jnp.float32)
    start = (code[0:1] * CODE + code[1:2]).astype(jnp.int32)
    dense = a_ref[0:slots, :].astype(jnp.float32)
    reach = slots
    for bit in range(max(1, (width - 1).bit_length())):
        step = 1 << bit
        reach = reach + step
        extent = min(width, -(-reach // 8) * 8)
        if extent > dense.shape[0]:
            dense = jnp.concatenate([dense, jnp.zeros((extent - dense.shape[0], lanes), jnp.float32)], axis=0)
        if step % 8 == 0:
            rolled = jnp.concatenate([dense[extent - step:], dense[: extent - step]], axis=0)
        else:
            rolled = pltpu.roll(dense, step, 0)
        dense = jnp.where(((start >> bit) & 1) == 1, rolled, dense)
    if dense.shape[0] < width:
        dense = jnp.concatenate([dense, jnp.zeros((width - dense.shape[0], lanes), jnp.float32)], axis=0)
    wave = jnp.dot(gt_ref[...], dense.astype(jnp.bfloat16), preferred_element_type=jnp.float32)
    rows = wave.shape[0]
    o_ref[...] = jnp.max(wave.reshape(rows // TSTEP, TSTEP, lanes), axis=1)


def wave_maxima(panel_t, coded):
    parts, height, lanes = coded.shape
    rows, width = panel_t.shape
    return pl.pallas_call(
        wave_kernel,
        grid=(parts,),
        in_specs=[
            pl.BlockSpec((rows, width), lambda p: (0, 0)),
            pl.BlockSpec((None, height, lanes), lambda p: (p, 0, 0)),
        ],
        out_specs=pl.BlockSpec((None, rows // TSTEP, lanes), lambda p: (p, 0, 0)),
        out_shape=jax.ShapeDtypeStruct((parts, rows // TSTEP, lanes), jnp.float32),
    )(panel_t, coded)


def shifted(values, step, fill):
    pad = jnp.full((abs(step),) + values.shape[1:], fill, values.dtype)
    if step > 0:
        return jnp.concatenate([pad, values[:-step]], axis=0)
    return jnp.concatenate([values[-step:], pad], axis=0)


def run_max(values, codes, reach, sign):
    step = 1
    while step < reach:
        other = shifted(values, sign * step, -jnp.inf)
        same = shifted(codes, sign * step, 0.0) == codes
        values = jnp.where(same, jnp.maximum(values, other), values)
        step *= 2
    return values


def point_peaks(window_max_t, win_point, reach):
    windows, scen = window_max_t.shape
    codes = (win_point + 1).astype(jnp.float32)[:, None]
    forward = run_max(window_max_t, codes, reach, 1)
    backward = run_max(window_max_t, codes, reach, -1)
    peak = jnp.maximum(forward, backward)
    count = lax.axis_size("rows")
    to_right = jnp.concatenate([forward[windows - 1:], jnp.broadcast_to(codes[windows - 1:], (1, scen))], axis=0)
    to_left = jnp.concatenate([backward[:1], jnp.broadcast_to(codes[:1], (1, scen))], axis=0)
    from_left = lax.ppermute(to_right, "rows", [(i, i + 1) for i in range(count - 1)])
    from_right = lax.ppermute(to_left, "rows", [(i + 1, i) for i in range(count - 1)])
    peak = jnp.where(codes == from_left[1:2], jnp.maximum(peak, from_left[0:1]), peak)
    peak = jnp.where(codes == from_right[1:2], jnp.maximum(peak, from_right[0:1]), peak)
    return peak.T


def local(greens, slip_values, rupture_ids, win_point):
    parts = lax.axis_size(SPLIT)
    shares = lax.axis_size(SHARE)
    own_sources, rows = greens.shape
    width = own_sources * parts * shares
    scen = slip_values.shape[0]
    block = rows // parts

    listed = rupture_ids >= 0
    values = jnp.where(listed, slip_values, jnp.zeros_like(slip_values))
    starts = jnp.maximum(rupture_ids[:, 0], 0)
    code = jnp.stack([starts // CODE, starts % CODE]).astype(jnp.bfloat16)
    coded = jnp.concatenate([values.T, code, jnp.zeros((14, scen), jnp.bfloat16)], axis=0)
    core = lax.rem(lax.axis_index("rows"), 2)
    half = scen // 2
    mine = lax.dynamic_slice_in_dim(coded, core * half, half, axis=1)
    mine = lax.all_gather(mine, SPLIT, axis=0, tiled=False)
    count_rows = lax.axis_size("rows")
    theirs = lax.ppermute(mine, "rows", [(i, i ^ 1) for i in range(count_rows)])
    coded = jnp.where(core == 0, jnp.concatenate([mine, theirs], axis=2), jnp.concatenate([theirs, mine], axis=2))

    pieces = greens.reshape(own_sources, parts, 1, block)
    pieces = jnp.broadcast_to(pieces, (own_sources, parts, shares, block)).reshape(own_sources, parts * shares, block)
    pieces = lax.all_to_all(pieces, COLS, 1, 0, tiled=True)
    panel_t = pieces.reshape(width, block).T

    maxima = wave_maxima(panel_t, coded)
    maxima = lax.all_to_all(maxima, SPLIT, 0, 0, tiled=True)
    return point_peaks(maxima.reshape(-1, scen), win_point, MOST)


def solution(mesh):
    split = Mesh(mesh.devices.reshape(mesh.shape["rows"], 8, 2), ("rows", "cols_0", "cols_1"))
    in_specs = (P(COLS, "rows"), P(COLS, None), P(COLS, None), P("rows"))
    out_specs = P(COLS, "rows")
    return jax.shard_map(local, mesh=split, in_specs=in_specs, out_specs=out_specs, check_vma=False)
```

```python
import jax
import jax.numpy as jnp
from jax import lax
from jax.experimental import pallas as pl
from jax.experimental.pallas import tpu as pltpu
from jax.sharding import Mesh
from jax.sharding import PartitionSpec as P

TSTEP = 64
COLS = ("cols_0", "cols_1")
SPLIT = "cols_0"
SHARE = "cols_1"
CODE = 32
MOST = 32


def wave_kernel(gt_ref, a_ref, o_ref):
    slots = a_ref.shape[0] - 16
    width = gt_ref.shape[1]
    lanes = a_ref.shape[1]
    code = a_ref[slots:slots + 16, :].astype(jnp.float32)
    start = (code[0:1] * CODE + code[1:2]).astype(jnp.int32)
    dense = a_ref[0:slots, :].astype(jnp.float32)
    reach = slots
    for bit in range(max(1, (width - 1).bit_length())):
        step = 1 << bit
        reach = reach + step
        extent = min(width, -(-reach // 8) * 8)
        if extent > dense.shape[0]:
            dense = jnp.concatenate([dense, jnp.zeros((extent - dense.shape[0], lanes), jnp.float32)], axis=0)
        if step % 8 == 0:
            rolled = jnp.concatenate([dense[extent - step:], dense[: extent - step]], axis=0)
        else:
            rolled = pltpu.roll(dense, step, 0)
        dense = jnp.where(((start >> bit) & 1) == 1, rolled, dense)
    if dense.shape[0] < width:
        dense = jnp.concatenate([dense, jnp.zeros((width - dense.shape[0], lanes), jnp.float32)], axis=0)
    wave = jnp.dot(gt_ref[...], dense.astype(jnp.bfloat16), preferred_element_type=jnp.float32)
    rows = wave.shape[0]
    o_ref[...] = jnp.max(wave.reshape(rows // TSTEP, TSTEP, lanes), axis=1)


def wave_maxima(panel_t, coded):
    parts, height, lanes = coded.shape
    rows, width = panel_t.shape
    return pl.pallas_call(
        wave_kernel,
        grid=(parts,),
        in_specs=[
            pl.BlockSpec((rows, width), lambda p: (0, 0)),
            pl.BlockSpec((None, height, lanes), lambda p: (p, 0, 0)),
        ],
        out_specs=pl.BlockSpec((None, rows // TSTEP, lanes), lambda p: (p, 0, 0)),
        out_shape=jax.ShapeDtypeStruct((parts, rows // TSTEP, lanes), jnp.float32),
    )(panel_t, coded)


def shifted(values, step, fill):
    pad = jnp.full((abs(step),) + values.shape[1:], fill, values.dtype)
    if step > 0:
        return jnp.concatenate([pad, values[:-step]], axis=0)
    return jnp.concatenate([values[-step:], pad], axis=0)


def run_max(values, codes, reach, sign):
    step = 1
    while step < reach:
        other = shifted(values, sign * step, -jnp.inf)
        same = shifted(codes, sign * step, 0.0) == codes
        values = jnp.where(same, jnp.maximum(values, other), values)
        step *= 2
    return values


def point_peaks(window_max_t, win_point, reach):
    windows, scen = window_max_t.shape
    codes = (win_point + 1).astype(jnp.float32)[:, None]
    forward = run_max(window_max_t, codes, reach, 1)
    backward = run_max(window_max_t, codes, reach, -1)
    peak = jnp.maximum(forward, backward)
    count = lax.axis_size("rows")
    to_right = jnp.concatenate([forward[windows - 1:], jnp.broadcast_to(codes[windows - 1:], (1, scen))], axis=0)
    to_left = jnp.concatenate([backward[:1], jnp.broadcast_to(codes[:1], (1, scen))], axis=0)
    from_left = lax.ppermute(to_right, "rows", [(i, i + 1) for i in range(count - 1)])
    from_right = lax.ppermute(to_left, "rows", [(i + 1, i) for i in range(count - 1)])
    peak = jnp.where(codes == from_left[1:2], jnp.maximum(peak, from_left[0:1]), peak)
    peak = jnp.where(codes == from_right[1:2], jnp.maximum(peak, from_right[0:1]), peak)
    return peak.T


def local(greens, slip_values, rupture_ids, win_point):
    parts = lax.axis_size(SPLIT)
    shares = lax.axis_size(SHARE)
    own_sources, rows = greens.shape
    width = own_sources * parts * shares
    scen = slip_values.shape[0]
    block = rows // parts

    listed = rupture_ids >= 0
    values = jnp.where(listed, slip_values, jnp.zeros_like(slip_values))
    starts = jnp.maximum(rupture_ids[:, 0], 0)
    code = jnp.stack([starts // CODE, starts % CODE]).astype(jnp.bfloat16)
    coded = jnp.concatenate([values.T, code, jnp.zeros((14, scen), jnp.bfloat16)], axis=0)
    core = lax.rem(lax.axis_index("rows"), 2)
    half = scen // 2
    mine = lax.dynamic_slice_in_dim(coded, core * half, half, axis=1)
    mine = jnp.broadcast_to(mine[None], (parts,) + mine.shape)
    mine = lax.all_to_all(mine, SPLIT, 0, 0, tiled=True)
    count_rows = lax.axis_size("rows")
    theirs = lax.ppermute(mine, "rows", [(i, i ^ 1) for i in range(count_rows)])
    coded = jnp.where(core == 0, jnp.concatenate([mine, theirs], axis=2), jnp.concatenate([theirs, mine], axis=2))

    pieces = greens.reshape(own_sources, parts, 1, block)
    pieces = jnp.broadcast_to(pieces, (own_sources, parts, shares, block)).reshape(own_sources, parts * shares, block)
    pieces = lax.all_to_all(pieces, COLS, 1, 0, tiled=True)
    panel_t = pieces.reshape(width, block).T

    maxima = wave_maxima(panel_t, coded)
    maxima = lax.all_to_all(maxima, SPLIT, 0, 0, tiled=True)
    return point_peaks(maxima.reshape(-1, scen), win_point, MOST)


def solution(mesh):
    split = Mesh(mesh.devices.reshape(mesh.shape["rows"], 8, 2), ("rows", "cols_0", "cols_1"))
    in_specs = (P(COLS, "rows"), P(COLS, None), P(COLS, None), P("rows"))
    out_specs = P(COLS, "rows")
    return jax.shard_map(local, mesh=split, in_specs=in_specs, out_specs=out_specs, check_vma=False)
```

```python
import jax
import jax.numpy as jnp
from jax import lax
from jax.experimental import pallas as pl
from jax.experimental.pallas import tpu as pltpu
from jax.sharding import Mesh
from jax.sharding import PartitionSpec as P

TSTEP = 64
COLS = ("cols_0", "cols_1")
SPLIT = "cols_0"
SHARE = "cols_1"
CODE = 32
MOST = 32


def wave_kernel(gt_ref, a_ref, o_ref):
    slots = a_ref.shape[0] - 16
    width = gt_ref.shape[1]
    lanes = a_ref.shape[1]
    code = a_ref[slots:slots + 16, :].astype(jnp.float32)
    start = (code[0:1] * CODE + code[1:2]).astype(jnp.int32)
    dense = a_ref[0:slots, :].astype(jnp.float32)
    reach = slots
    for bit in range(max(1, (width - 1).bit_length())):
        step = 1 << bit
        reach = reach + step
        extent = min(width, -(-reach // 8) * 8)
        if extent > dense.shape[0]:
            dense = jnp.concatenate([dense, jnp.zeros((extent - dense.shape[0], lanes), jnp.float32)], axis=0)
        if step % 8 == 0:
            rolled = jnp.concatenate([dense[extent - step:], dense[: extent - step]], axis=0)
        else:
            rolled = pltpu.roll(dense, step, 0)
        dense = jnp.where(((start >> bit) & 1) == 1, rolled, dense)
    if dense.shape[0] < width:
        dense = jnp.concatenate([dense, jnp.zeros((width - dense.shape[0], lanes), jnp.float32)], axis=0)
    wave = jnp.dot(gt_ref[...], dense.astype(jnp.bfloat16), preferred_element_type=jnp.float32)
    rows = wave.shape[0]
    o_ref[...] = jnp.max(wave.reshape(rows // TSTEP, TSTEP, lanes), axis=1)


def wave_maxima(panel_t, coded):
    parts, height, lanes = coded.shape
    rows, width = panel_t.shape
    return pl.pallas_call(
        wave_kernel,
        grid=(parts,),
        in_specs=[
            pl.BlockSpec((rows, width), lambda p: (0, 0)),
            pl.BlockSpec((None, height, lanes), lambda p: (p, 0, 0)),
        ],
        out_specs=pl.BlockSpec((None, rows // TSTEP, lanes), lambda p: (p, 0, 0)),
        out_shape=jax.ShapeDtypeStruct((parts, rows // TSTEP, lanes), jnp.float32),
    )(panel_t, coded)


def shifted(values, step, fill):
    pad = jnp.full((abs(step),) + values.shape[1:], fill, values.dtype)
    if step > 0:
        return jnp.concatenate([pad, values[:-step]], axis=0)
    return jnp.concatenate([values[-step:], pad], axis=0)


def run_max(values, codes, reach, sign):
    step = 1
    while step < reach:
        other = shifted(values, sign * step, -jnp.inf)
        same = shifted(codes, sign * step, 0.0) == codes
        values = jnp.where(same, jnp.maximum(values, other), values)
        step *= 2
    return values


def point_peaks(window_max_t, win_point, reach):
    windows, scen = window_max_t.shape
    codes = (win_point + 1).astype(jnp.float32)[:, None]
    forward = run_max(window_max_t, codes, reach, 1)
    backward = run_max(window_max_t, codes, reach, -1)
    peak = jnp.maximum(forward, backward)
    count = lax.axis_size("rows")
    to_right = jnp.concatenate([forward[windows - 1:], jnp.broadcast_to(codes[windows - 1:], (1, scen))], axis=0)
    to_left = jnp.concatenate([backward[:1], jnp.broadcast_to(codes[:1], (1, scen))], axis=0)
    from_left = lax.ppermute(to_right, "rows", [(i, i + 1) for i in range(count - 1)])
    from_right = lax.ppermute(to_left, "rows", [(i + 1, i) for i in range(count - 1)])
    peak = jnp.where(codes == from_left[1:2], jnp.maximum(peak, from_left[0:1]), peak)
    peak = jnp.where(codes == from_right[1:2], jnp.maximum(peak, from_right[0:1]), peak)
    return peak.T


def local(greens, slip_values, rupture_ids, win_point):
    parts = lax.axis_size(SPLIT)
    shares = lax.axis_size(SHARE)
    own_sources, rows = greens.shape
    width = own_sources * parts * shares
    scen = slip_values.shape[0]
    block = rows // parts

    listed = rupture_ids >= 0
    values = jnp.where(listed, slip_values, jnp.zeros_like(slip_values))
    starts = jnp.maximum(rupture_ids[:, 0], 0)
    code = jnp.stack([starts // CODE, starts % CODE]).astype(jnp.bfloat16)
    coded = jnp.concatenate([values.T, code, jnp.zeros((14, scen), jnp.bfloat16)], axis=0)
    core = lax.rem(lax.axis_index("rows"), 2)
    side = lax.axis_index(SHARE)
    half = scen // 2
    mine = lax.dynamic_slice_in_dim(coded, core * half, half, axis=1)
    height = mine.shape[0]
    outgoing = jnp.concatenate(
        [
            greens.reshape(own_sources, parts, block).transpose(1, 0, 2),
            jnp.broadcast_to(mine.reshape(1, -1, block), (parts, height * half // block, block)),
        ],
        axis=1,
    )
    incoming = lax.all_to_all(outgoing, SPLIT, 0, 0, tiled=True)
    near = incoming[:, :own_sources]
    mine = incoming[:, own_sources:].reshape(parts, height, half)
    count_rows = lax.axis_size("rows")
    far = lax.ppermute(near, SHARE, [(i, (i + 1) % shares) for i in range(shares)])
    theirs = lax.ppermute(mine, "rows", [(i, i ^ 1) for i in range(count_rows)])
    coded = jnp.where(core == 0, jnp.concatenate([mine, theirs], axis=2), jnp.concatenate([theirs, mine], axis=2))
    panel = jnp.where(side == 0, jnp.stack([near, far], axis=1), jnp.stack([far, near], axis=1))
    panel_t = panel.reshape(width, block).T

    maxima = wave_maxima(panel_t, coded)
    maxima = lax.all_to_all(maxima, SPLIT, 0, 0, tiled=True)
    return point_peaks(maxima.reshape(-1, scen), win_point, MOST)


def solution(mesh):
    split = Mesh(mesh.devices.reshape(mesh.shape["rows"], 8, 2), ("rows", "cols_0", "cols_1"))
    in_specs = (P(COLS, "rows"), P(COLS, None), P(COLS, None), P("rows"))
    out_specs = P(COLS, "rows")
    return jax.shard_map(local, mesh=split, in_specs=in_specs, out_specs=out_specs, check_vma=False)
```

```python
import jax
import jax.numpy as jnp
from jax import lax
from jax.experimental import pallas as pl
from jax.experimental.pallas import tpu as pltpu
from jax.sharding import Mesh
from jax.sharding import PartitionSpec as P


TSTEP = 64
COLS = ("cols_0", "cols_1")
SPLIT = "cols_0"
SHARE = "cols_1"
CODE = 32
MOST = 32


def dense_kernel(a_ref, d_ref):
    slots = a_ref.shape[0] - 16
    width = d_ref.shape[0]
    lanes = a_ref.shape[1]
    code = a_ref[slots:slots + 16, :].astype(jnp.float32)
    start = (code[0:1] * CODE + code[1:2]).astype(jnp.int32)
    dense = a_ref[0:slots, :].astype(jnp.float32)
    reach = slots
    for bit in range(max(1, (width - 1).bit_length())):
        step = 1 << bit
        reach = reach + step
        extent = min(width, -(-reach // 8) * 8)
        if extent > dense.shape[0]:
            dense = jnp.concatenate([dense, jnp.zeros((extent - dense.shape[0], lanes), jnp.float32)], axis=0)
        if step % 8 == 0:
            rolled = jnp.concatenate([dense[extent - step:], dense[: extent - step]], axis=0)
        else:
            rolled = pltpu.roll(dense, step, 0)
        dense = jnp.where(((start >> bit) & 1) == 1, rolled, dense)
    if dense.shape[0] < width:
        dense = jnp.concatenate([dense, jnp.zeros((width - dense.shape[0], lanes), jnp.float32)], axis=0)
    d_ref[...] = dense.astype(d_ref.dtype)


def dense_slips(coded, width):
    parts, height, lanes = coded.shape
    return pl.pallas_call(
        dense_kernel,
        grid=(parts,),
        in_specs=[pl.BlockSpec((None, height, lanes), lambda p: (p, 0, 0))],
        out_specs=pl.BlockSpec((None, width, lanes), lambda p: (p, 0, 0)),
        out_shape=jax.ShapeDtypeStruct((parts, width, lanes), jnp.bfloat16),
    )(coded)


def wave_kernel(gt_ref, d_ref, o_ref):
    wave = jnp.dot(gt_ref[...], d_ref[...], preferred_element_type=jnp.float32)
    rows, lanes = wave.shape
    o_ref[...] = jnp.max(wave.reshape(rows // TSTEP, TSTEP, lanes), axis=1)


def wave_maxima(panel_t, dense):
    parts, width, lanes = dense.shape
    rows = panel_t.shape[0]
    return pl.pallas_call(
        wave_kernel,
        grid=(parts,),
        in_specs=[
            pl.BlockSpec((rows, width), lambda p: (0, 0)),
            pl.BlockSpec((None, width, lanes), lambda p: (p, 0, 0)),
        ],
        out_specs=pl.BlockSpec((None, rows // TSTEP, lanes), lambda p: (p, 0, 0)),
        out_shape=jax.ShapeDtypeStruct((parts, rows // TSTEP, lanes), jnp.float32),
    )(panel_t, dense)


def shifted(values, step, fill):
    pad = jnp.full((abs(step),) + values.shape[1:], fill, values.dtype)
    if step > 0:
        return jnp.concatenate([pad, values[:-step]], axis=0)
    return jnp.concatenate([values[-step:], pad], axis=0)


def run_max(values, codes, reach, sign):
    step = 1
    while step < reach:
        other = shifted(values, sign * step, -jnp.inf)
        same = shifted(codes, sign * step, 0.0) == codes
        values = jnp.where(same, jnp.maximum(values, other), values)
        step *= 2
    return values


def point_peaks(window_max_t, win_point, reach):
    windows, scen = window_max_t.shape
    codes = (win_point + 1).astype(jnp.float32)[:, None]
    forward = run_max(window_max_t, codes, reach, 1)
    backward = run_max(window_max_t, codes, reach, -1)
    peak = jnp.maximum(forward, backward)
    count = lax.axis_size("rows")
    to_right = jnp.concatenate([forward[windows - 1:], jnp.broadcast_to(codes[windows - 1:], (1, scen))], axis=0)
    to_left = jnp.concatenate([backward[:1], jnp.broadcast_to(codes[:1], (1, scen))], axis=0)
    from_left = lax.ppermute(to_right, "rows", [(i, i + 1) for i in range(count - 1)])
    from_right = lax.ppermute(to_left, "rows", [(i + 1, i) for i in range(count - 1)])
    peak = jnp.where(codes == from_left[1:2], jnp.maximum(peak, from_left[0:1]), peak)
    peak = jnp.where(codes == from_right[1:2], jnp.maximum(peak, from_right[0:1]), peak)
    return peak.T


def step(greens, slip_values, rupture_ids, win_point):
    parts = lax.axis_size(SPLIT)
    shares = lax.axis_size(SHARE)
    own_sources, rows = greens.shape
    width = own_sources * parts * shares
    scen = slip_values.shape[0]
    block = rows // parts

    listed = rupture_ids >= 0
    values = jnp.where(listed, slip_values, jnp.zeros_like(slip_values))
    starts = jnp.maximum(rupture_ids[:, 0], 0)
    code = jnp.stack([starts // CODE, starts % CODE]).astype(jnp.bfloat16)
    coded = jnp.concatenate([values.T, code, jnp.zeros((14, scen), jnp.bfloat16)], axis=0)
    core = lax.rem(lax.axis_index("rows"), 2)
    side = lax.axis_index(SHARE)
    half = scen // 2
    mine = lax.dynamic_slice_in_dim(coded, core * half, half, axis=1)
    height = mine.shape[0]
    outgoing = jnp.concatenate(
        [
            greens.reshape(own_sources, parts, block).transpose(1, 0, 2),
            jnp.broadcast_to(mine.reshape(1, -1, block), (parts, height * half // block, block)),
        ],
        axis=1,
    )
    incoming = lax.all_to_all(outgoing, SPLIT, 0, 0, tiled=True)
    near = incoming[:, :own_sources]
    mine = incoming[:, own_sources:].reshape(parts, height, half)
    count_rows = lax.axis_size("rows")
    far = lax.ppermute(near, SHARE, [(i, (i + 1) % shares) for i in range(shares)])
    theirs = lax.ppermute(mine, "rows", [(i, i ^ 1) for i in range(count_rows)])
    coded = jnp.where(core == 0, jnp.concatenate([mine, theirs], axis=2), jnp.concatenate([theirs, mine], axis=2))
    dense = dense_slips(coded, width)
    panel = jnp.where(side == 0, jnp.stack([near, far], axis=1), jnp.stack([far, near], axis=1))
    panel_t = panel.reshape(width, block).T

    maxima = wave_maxima(panel_t, dense)
    maxima = lax.all_to_all(maxima, SPLIT, 0, 0, tiled=True)
    return point_peaks(maxima.reshape(-1, scen), win_point, MOST)


def solution(mesh):
    split = Mesh(mesh.devices.reshape(mesh.shape["rows"], 8, 2), ("rows", "cols_0", "cols_1"))
    in_specs = (P(COLS, "rows"), P(COLS, None), P(COLS, None), P("rows"))
    out_specs = P(COLS, "rows")
    return jax.shard_map(step, mesh=split, in_specs=in_specs, out_specs=out_specs, check_vma=False)
```

```python
import jax
import jax.numpy as jnp
from jax import lax
from jax.experimental import pallas as pl
from jax.experimental.pallas import tpu as pltpu
from jax.sharding import Mesh
from jax.sharding import PartitionSpec as P


TSTEP = 64
COLS = ("cols_0", "cols_1")
SPLIT = "cols_0"
SHARE = "cols_1"
CODE = 32
MOST = 32


def dense_kernel(a_ref, d_ref):
    slots = a_ref.shape[0] - 16
    width = d_ref.shape[0]
    lanes = a_ref.shape[1]
    code = a_ref[slots:slots + 16, :].astype(jnp.float32)
    start = (code[0:1] * CODE + code[1:2]).astype(jnp.int32)
    dense = a_ref[0:slots, :].astype(jnp.float32)
    reach = slots
    for bit in range(max(1, (width - 1).bit_length())):
        step = 1 << bit
        reach = reach + step
        extent = min(width, -(-reach // 8) * 8)
        if extent > dense.shape[0]:
            dense = jnp.concatenate([dense, jnp.zeros((extent - dense.shape[0], lanes), jnp.float32)], axis=0)
        if step % 8 == 0:
            rolled = jnp.concatenate([dense[extent - step:], dense[: extent - step]], axis=0)
        else:
            rolled = pltpu.roll(dense, step, 0)
        dense = jnp.where(((start >> bit) & 1) == 1, rolled, dense)
    if dense.shape[0] < width:
        dense = jnp.concatenate([dense, jnp.zeros((width - dense.shape[0], lanes), jnp.float32)], axis=0)
    d_ref[...] = dense.astype(d_ref.dtype)


def dense_slips(coded, width):
    parts, height, lanes = coded.shape
    return pl.pallas_call(
        dense_kernel,
        grid=(parts,),
        in_specs=[pl.BlockSpec((None, height, lanes), lambda p: (p, 0, 0))],
        out_specs=pl.BlockSpec((None, width, lanes), lambda p: (p, 0, 0)),
        out_shape=jax.ShapeDtypeStruct((parts, width, lanes), jnp.bfloat16),
    )(coded)


def wave_kernel(gt_ref, d_ref, o_ref):
    dense = d_ref[...]
    rows = gt_ref.shape[0]
    group = min(8, rows // TSTEP)
    for first in range(0, rows // TSTEP, group):
        wave = jnp.dot(gt_ref[first * TSTEP:(first + group) * TSTEP, :], dense, preferred_element_type=jnp.float32)
        peaks = [jnp.max(wave[w * TSTEP:(w + 1) * TSTEP], axis=0, keepdims=True) for w in range(group)]
        o_ref[first:first + group, :] = jnp.concatenate(peaks, axis=0)


def wave_maxima(panel_t, dense):
    parts, width, lanes = dense.shape
    rows = panel_t.shape[0]
    return pl.pallas_call(
        wave_kernel,
        grid=(parts,),
        in_specs=[
            pl.BlockSpec((rows, width), lambda p: (0, 0)),
            pl.BlockSpec((None, width, lanes), lambda p: (p, 0, 0)),
        ],
        out_specs=pl.BlockSpec((None, rows // TSTEP, lanes), lambda p: (p, 0, 0)),
        out_shape=jax.ShapeDtypeStruct((parts, rows // TSTEP, lanes), jnp.float32),
    )(panel_t, dense)


def shifted(values, step, fill):
    pad = jnp.full((abs(step),) + values.shape[1:], fill, values.dtype)
    if step > 0:
        return jnp.concatenate([pad, values[:-step]], axis=0)
    return jnp.concatenate([values[-step:], pad], axis=0)


def run_max(values, codes, reach, sign):
    step = 1
    while step < reach:
        other = shifted(values, sign * step, -jnp.inf)
        same = shifted(codes, sign * step, 0.0) == codes
        values = jnp.where(same, jnp.maximum(values, other), values)
        step *= 2
    return values


def point_peaks(window_max_t, win_point, reach):
    windows, scen = window_max_t.shape
    codes = (win_point + 1).astype(jnp.float32)[:, None]
    forward = run_max(window_max_t, codes, reach, 1)
    backward = run_max(window_max_t, codes, reach, -1)
    peak = jnp.maximum(forward, backward)
    count = lax.axis_size("rows")
    to_right = jnp.concatenate([forward[windows - 1:], jnp.broadcast_to(codes[windows - 1:], (1, scen))], axis=0)
    to_left = jnp.concatenate([backward[:1], jnp.broadcast_to(codes[:1], (1, scen))], axis=0)
    from_left = lax.ppermute(to_right, "rows", [(i, i + 1) for i in range(count - 1)])
    from_right = lax.ppermute(to_left, "rows", [(i + 1, i) for i in range(count - 1)])
    peak = jnp.where(codes == from_left[1:2], jnp.maximum(peak, from_left[0:1]), peak)
    peak = jnp.where(codes == from_right[1:2], jnp.maximum(peak, from_right[0:1]), peak)
    return peak.T


def step(greens, slip_values, rupture_ids, win_point):
    parts = lax.axis_size(SPLIT)
    shares = lax.axis_size(SHARE)
    own_sources, rows = greens.shape
    width = own_sources * parts * shares
    scen = slip_values.shape[0]
    block = rows // parts

    listed = rupture_ids >= 0
    values = jnp.where(listed, slip_values, jnp.zeros_like(slip_values))
    starts = jnp.maximum(rupture_ids[:, 0], 0)
    code = jnp.stack([starts // CODE, starts % CODE]).astype(jnp.bfloat16)
    coded = jnp.concatenate([values.T, code, jnp.zeros((14, scen), jnp.bfloat16)], axis=0)
    core = lax.rem(lax.axis_index("rows"), 2)
    side = lax.axis_index(SHARE)
    half = scen // 2
    mine = lax.dynamic_slice_in_dim(coded, core * half, half, axis=1)
    height = mine.shape[0]
    outgoing = jnp.concatenate(
        [
            greens.reshape(own_sources, parts, block).transpose(1, 0, 2),
            jnp.broadcast_to(mine.reshape(1, -1, block), (parts, height * half // block, block)),
        ],
        axis=1,
    )
    incoming = lax.all_to_all(outgoing, SPLIT, 0, 0, tiled=True)
    near = incoming[:, :own_sources]
    mine = incoming[:, own_sources:].reshape(parts, height, half)
    count_rows = lax.axis_size("rows")
    far = lax.ppermute(near, SHARE, [(i, (i + 1) % shares) for i in range(shares)])
    theirs = lax.ppermute(mine, "rows", [(i, i ^ 1) for i in range(count_rows)])
    coded = jnp.where(core == 0, jnp.concatenate([mine, theirs], axis=2), jnp.concatenate([theirs, mine], axis=2))
    dense = dense_slips(coded, width)
    panel = jnp.where(side == 0, jnp.stack([near, far], axis=1), jnp.stack([far, near], axis=1))
    panel_t = panel.reshape(width, block).T

    maxima = wave_maxima(panel_t, dense)
    maxima = lax.all_to_all(maxima, SPLIT, 0, 0, tiled=True)
    return point_peaks(maxima.reshape(-1, scen), win_point, MOST)


def solution(mesh):
    split = Mesh(mesh.devices.reshape(mesh.shape["rows"], 8, 2), ("rows", "cols_0", "cols_1"))
    in_specs = (P(COLS, "rows"), P(COLS, None), P(COLS, None), P("rows"))
    out_specs = P(COLS, "rows")
    return jax.shard_map(step, mesh=split, in_specs=in_specs, out_specs=out_specs, check_vma=False)
```

```python
import jax
import jax.numpy as jnp
from jax import lax
from jax.experimental import pallas as pl
from jax.experimental.pallas import tpu as pltpu
from jax.sharding import Mesh
from jax.sharding import PartitionSpec as P


TSTEP = 64
COLS = ("cols_0", "cols_1")
SPLIT = "cols_0"
SHARE = "cols_1"
CODE = 32
MOST = 32


def dense_kernel(a_ref, d_ref):
    slots = a_ref.shape[0] - 16
    width = d_ref.shape[0]
    lanes = a_ref.shape[1]
    code = a_ref[slots:slots + 16, :].astype(jnp.float32)
    start = (code[0:1] * CODE + code[1:2]).astype(jnp.int32)
    dense = a_ref[0:slots, :].astype(jnp.float32)
    reach = slots
    for bit in range(max(1, (width - 1).bit_length())):
        step = 1 << bit
        reach = reach + step
        extent = min(width, -(-reach // 8) * 8)
        if extent > dense.shape[0]:
            dense = jnp.concatenate([dense, jnp.zeros((extent - dense.shape[0], lanes), jnp.float32)], axis=0)
        if step % 8 == 0:
            rolled = jnp.concatenate([dense[extent - step:], dense[: extent - step]], axis=0)
        else:
            rolled = pltpu.roll(dense, step, 0)
        dense = jnp.where(((start >> bit) & 1) == 1, rolled, dense)
    if dense.shape[0] < width:
        dense = jnp.concatenate([dense, jnp.zeros((width - dense.shape[0], lanes), jnp.float32)], axis=0)
    d_ref[...] = dense.astype(d_ref.dtype)


def dense_slips(coded, width):
    parts, height, lanes = coded.shape
    return pl.pallas_call(
        dense_kernel,
        grid=(parts,),
        in_specs=[pl.BlockSpec((None, height, lanes), lambda p: (p, 0, 0))],
        out_specs=pl.BlockSpec((None, width, lanes), lambda p: (p, 0, 0)),
        out_shape=jax.ShapeDtypeStruct((parts, width, lanes), jnp.bfloat16),
    )(coded)


def near_kernel(gt_ref, d_ref, o_ref):
    o_ref[...] = jnp.dot(gt_ref[...], d_ref[...], preferred_element_type=jnp.float32)


def near_waves(panel_t, dense):
    parts, width, lanes = dense.shape
    rows = panel_t.shape[0]
    return pl.pallas_call(
        near_kernel,
        grid=(parts,),
        in_specs=[
            pl.BlockSpec((rows, width), lambda p: (0, 0)),
            pl.BlockSpec((None, width, lanes), lambda p: (p, 0, 0)),
        ],
        out_specs=pl.BlockSpec((None, rows, lanes), lambda p: (p, 0, 0)),
        out_shape=jax.ShapeDtypeStruct((parts, rows, lanes), jnp.float32),
    )(panel_t, dense)


def wave_kernel(gt_ref, d_ref, w_ref, o_ref):
    wave = w_ref[...] + jnp.dot(gt_ref[...], d_ref[...], preferred_element_type=jnp.float32)
    rows, lanes = wave.shape
    o_ref[...] = jnp.max(wave.reshape(rows // TSTEP, TSTEP, lanes), axis=1)


def wave_maxima(panel_t, dense, partial):
    parts, width, lanes = dense.shape
    rows = panel_t.shape[0]
    return pl.pallas_call(
        wave_kernel,
        grid=(parts,),
        in_specs=[
            pl.BlockSpec((rows, width), lambda p: (0, 0)),
            pl.BlockSpec((None, width, lanes), lambda p: (p, 0, 0)),
            pl.BlockSpec((None, rows, lanes), lambda p: (p, 0, 0)),
        ],
        out_specs=pl.BlockSpec((None, rows // TSTEP, lanes), lambda p: (p, 0, 0)),
        out_shape=jax.ShapeDtypeStruct((parts, rows // TSTEP, lanes), jnp.float32),
    )(panel_t, dense, partial)


def shifted(values, step, fill):
    pad = jnp.full((abs(step),) + values.shape[1:], fill, values.dtype)
    if step > 0:
        return jnp.concatenate([pad, values[:-step]], axis=0)
    return jnp.concatenate([values[-step:], pad], axis=0)


def run_max(values, codes, reach, sign):
    step = 1
    while step < reach:
        other = shifted(values, sign * step, -jnp.inf)
        same = shifted(codes, sign * step, 0.0) == codes
        values = jnp.where(same, jnp.maximum(values, other), values)
        step *= 2
    return values


def point_peaks(window_max_t, win_point, reach):
    windows, scen = window_max_t.shape
    codes = (win_point + 1).astype(jnp.float32)[:, None]
    forward = run_max(window_max_t, codes, reach, 1)
    backward = run_max(window_max_t, codes, reach, -1)
    peak = jnp.maximum(forward, backward)
    count = lax.axis_size("rows")
    to_right = jnp.concatenate([forward[windows - 1:], jnp.broadcast_to(codes[windows - 1:], (1, scen))], axis=0)
    to_left = jnp.concatenate([backward[:1], jnp.broadcast_to(codes[:1], (1, scen))], axis=0)
    from_left = lax.ppermute(to_right, "rows", [(i, i + 1) for i in range(count - 1)])
    from_right = lax.ppermute(to_left, "rows", [(i + 1, i) for i in range(count - 1)])
    peak = jnp.where(codes == from_left[1:2], jnp.maximum(peak, from_left[0:1]), peak)
    peak = jnp.where(codes == from_right[1:2], jnp.maximum(peak, from_right[0:1]), peak)
    return peak.T


def step(greens, slip_values, rupture_ids, win_point):
    parts = lax.axis_size(SPLIT)
    shares = lax.axis_size(SHARE)
    own_sources, rows = greens.shape
    width = own_sources * parts * shares
    scen = slip_values.shape[0]
    block = rows // parts

    listed = rupture_ids >= 0
    values = jnp.where(listed, slip_values, jnp.zeros_like(slip_values))
    starts = jnp.maximum(rupture_ids[:, 0], 0)
    code = jnp.stack([starts // CODE, starts % CODE]).astype(jnp.bfloat16)
    coded = jnp.concatenate([values.T, code, jnp.zeros((14, scen), jnp.bfloat16)], axis=0)
    core = lax.rem(lax.axis_index("rows"), 2)
    side = lax.axis_index(SHARE)
    half = scen // 2
    mine = lax.dynamic_slice_in_dim(coded, core * half, half, axis=1)
    height = mine.shape[0]
    outgoing = jnp.concatenate(
        [
            greens.reshape(own_sources, parts, block).transpose(1, 0, 2),
            jnp.broadcast_to(mine.reshape(1, -1, block), (parts, height * half // block, block)),
        ],
        axis=1,
    )
    incoming = lax.all_to_all(outgoing, SPLIT, 0, 0, tiled=True)
    near = incoming[:, :own_sources]
    mine = incoming[:, own_sources:].reshape(parts, height, half)
    count_rows = lax.axis_size("rows")
    far = lax.ppermute(near, SHARE, [(i, (i + 1) % shares) for i in range(shares)])
    theirs = lax.ppermute(mine, "rows", [(i, i ^ 1) for i in range(count_rows)])
    coded = jnp.where(core == 0, jnp.concatenate([mine, theirs], axis=2), jnp.concatenate([theirs, mine], axis=2))
    dense = dense_slips(coded, width)
    dense = dense.reshape(parts, parts, shares, own_sources, scen)
    dense_near = jnp.where(side == 0, dense[:, :, 0], dense[:, :, 1]).reshape(parts, width // shares, scen)
    dense_far = jnp.where(side == 0, dense[:, :, 1], dense[:, :, 0]).reshape(parts, width // shares, scen)
    partial = near_waves(near.reshape(width // shares, block).T, dense_near)
    maxima = wave_maxima(far.reshape(width // shares, block).T, dense_far, partial)
    maxima = lax.all_to_all(maxima, SPLIT, 0, 0, tiled=True)
    return point_peaks(maxima.reshape(-1, scen), win_point, MOST)


def solution(mesh):
    split = Mesh(mesh.devices.reshape(mesh.shape["rows"], 8, 2), ("rows", "cols_0", "cols_1"))
    in_specs = (P(COLS, "rows"), P(COLS, None), P(COLS, None), P("rows"))
    out_specs = P(COLS, "rows")
    return jax.shard_map(step, mesh=split, in_specs=in_specs, out_specs=out_specs, check_vma=False)
```

```python
import jax
import jax.numpy as jnp
from jax import lax
from jax.experimental import pallas as pl
from jax.experimental.pallas import tpu as pltpu
from jax.sharding import Mesh
from jax.sharding import PartitionSpec as P

TSTEP = 64
COLS = ("cols_0", "cols_1")
SPLIT = "cols_0"
SHARE = "cols_1"
CODE = 32
MOST = 32


def wave_kernel(gt_ref, a_ref, o_ref):
    slots = a_ref.shape[0] - 16
    width = gt_ref.shape[1]
    lanes = a_ref.shape[1]
    code = a_ref[slots:slots + 16, :].astype(jnp.float32)
    start = (code[0:1] * CODE + code[1:2]).astype(jnp.int32)
    dense = a_ref[0:slots, :].astype(jnp.float32)
    reach = slots
    for bit in range(max(1, (width - 1).bit_length())):
        step = 1 << bit
        reach = reach + step
        extent = min(width, -(-reach // 8) * 8)
        if extent > dense.shape[0]:
            dense = jnp.concatenate([dense, jnp.zeros((extent - dense.shape[0], lanes), jnp.float32)], axis=0)
        if step % 8 == 0:
            rolled = jnp.concatenate([dense[extent - step:], dense[: extent - step]], axis=0)
        else:
            rolled = pltpu.roll(dense, step, 0)
        dense = jnp.where(((start >> bit) & 1) == 1, rolled, dense)
    if dense.shape[0] < width:
        dense = jnp.concatenate([dense, jnp.zeros((width - dense.shape[0], lanes), jnp.float32)], axis=0)
    wave = jnp.dot(gt_ref[...], dense.astype(jnp.bfloat16), preferred_element_type=jnp.float32)
    rows = wave.shape[0]
    o_ref[...] = jnp.max(wave.reshape(rows // TSTEP, TSTEP, lanes), axis=1)


def wave_maxima(panel_t, coded):
    parts, height, lanes = coded.shape
    rows, width = panel_t.shape
    return pl.pallas_call(
        wave_kernel,
        grid=(parts,),
        in_specs=[
            pl.BlockSpec((rows, width), lambda p: (0, 0)),
            pl.BlockSpec((None, height, lanes), lambda p: (p, 0, 0)),
        ],
        out_specs=pl.BlockSpec((None, rows // TSTEP, lanes), lambda p: (p, 0, 0)),
        out_shape=jax.ShapeDtypeStruct((parts, rows // TSTEP, lanes), jnp.float32),
    )(panel_t, coded)


def shifted(values, step, fill):
    pad = jnp.full((abs(step),) + values.shape[1:], fill, values.dtype)
    if step > 0:
        return jnp.concatenate([pad, values[:-step]], axis=0)
    return jnp.concatenate([values[-step:], pad], axis=0)


def run_max(values, codes, reach, sign):
    step = 1
    while step < reach:
        other = shifted(values, sign * step, -jnp.inf)
        same = shifted(codes, sign * step, 0.0) == codes
        values = jnp.where(same, jnp.maximum(values, other), values)
        step *= 2
    return values


def point_peaks(window_max_t, win_point, reach):
    windows, scen = window_max_t.shape
    codes = (win_point + 1).astype(jnp.float32)[:, None]
    forward = run_max(window_max_t, codes, reach, 1)
    backward = run_max(window_max_t, codes, reach, -1)
    peak = jnp.maximum(forward, backward)
    count = lax.axis_size("rows")
    to_right = jnp.concatenate([forward[windows - 1:], jnp.broadcast_to(codes[windows - 1:], (1, scen))], axis=0)
    to_left = jnp.concatenate([backward[:1], jnp.broadcast_to(codes[:1], (1, scen))], axis=0)
    from_left = lax.ppermute(to_right, "rows", [(i, i + 1) for i in range(count - 1)])
    from_right = lax.ppermute(to_left, "rows", [(i + 1, i) for i in range(count - 1)])
    peak = jnp.where(codes == from_left[1:2], jnp.maximum(peak, from_left[0:1]), peak)
    peak = jnp.where(codes == from_right[1:2], jnp.maximum(peak, from_right[0:1]), peak)
    return peak.T


def local(greens, slip_values, rupture_ids, win_point):
    parts = lax.axis_size(SPLIT)
    shares = lax.axis_size(SHARE)
    own_sources, rows = greens.shape
    width = own_sources * parts * shares
    scen = slip_values.shape[0]
    block = rows // parts

    listed = rupture_ids >= 0
    values = jnp.where(listed, slip_values, jnp.zeros_like(slip_values))
    starts = jnp.maximum(rupture_ids[:, 0], 0)
    code = jnp.stack([starts // CODE, starts % CODE]).astype(jnp.bfloat16)
    coded = jnp.concatenate([values.T, code, jnp.zeros((14, scen), jnp.bfloat16)], axis=0)
    core = lax.rem(lax.axis_index("rows"), 2)
    side = lax.axis_index(SHARE)
    half = scen // 2
    mine = lax.dynamic_slice_in_dim(coded, core * half, half, axis=1)
    height = mine.shape[0]
    greens_part = greens.reshape(own_sources, parts, block).transpose(1, 0, 2).reshape(parts, own_sources * block)
    slips_part = jnp.broadcast_to(mine.reshape(1, height * half), (parts, height * half))
    message = own_sources * block + height * half
    lanes = message // 16 if message % (16 * 128) == 0 else message
    outgoing = jnp.concatenate([greens_part, slips_part], axis=1).reshape(parts, message // lanes, lanes)
    incoming = lax.all_to_all(outgoing, SPLIT, 0, 0, tiled=True).reshape(parts, message)
    near = incoming[:, : own_sources * block].reshape(parts, own_sources, block)
    mine = incoming[:, own_sources * block:].reshape(parts, height, half)
    count_rows = lax.axis_size("rows")
    far = lax.ppermute(near, SHARE, [(i, (i + 1) % shares) for i in range(shares)])
    theirs = lax.ppermute(mine, "rows", [(i, i ^ 1) for i in range(count_rows)])
    coded = jnp.where(core == 0, jnp.concatenate([mine, theirs], axis=2), jnp.concatenate([theirs, mine], axis=2))
    panel = jnp.where(side == 0, jnp.stack([near, far], axis=1), jnp.stack([far, near], axis=1))
    panel_t = panel.reshape(width, block).T

    maxima = wave_maxima(panel_t, coded)
    maxima = lax.all_to_all(maxima, SPLIT, 0, 0, tiled=True)
    return point_peaks(maxima.reshape(-1, scen), win_point, MOST)


def solution(mesh):
    split = Mesh(mesh.devices.reshape(mesh.shape["rows"], 8, 2), ("rows", "cols_0", "cols_1"))
    in_specs = (P(COLS, "rows"), P(COLS, None), P(COLS, None), P("rows"))
    out_specs = P(COLS, "rows")
    return jax.shard_map(local, mesh=split, in_specs=in_specs, out_specs=out_specs, check_vma=False)
```

```python
import jax
import jax.numpy as jnp
from jax import lax
from jax.experimental import pallas as pl
from jax.experimental.pallas import tpu as pltpu
from jax.sharding import Mesh
from jax.sharding import PartitionSpec as P

TSTEP = 64
COLS = ("cols_0", "cols_1")
SPLIT = "cols_0"
SHARE = "cols_1"
CODE = 32
MOST = 32


def wave_kernel(gt_ref, a_ref, o_ref):
    slots = a_ref.shape[0] - 16
    width = gt_ref.shape[1]
    lanes = a_ref.shape[1]
    code = a_ref[slots:slots + 16, :].astype(jnp.float32)
    start = (code[0:1] * CODE + code[1:2]).astype(jnp.int32)
    dense = a_ref[0:slots, :].astype(jnp.float32)
    reach = slots
    for bit in range(max(1, (width - 1).bit_length())):
        step = 1 << bit
        reach = reach + step
        extent = min(width, -(-reach // 8) * 8)
        if extent > dense.shape[0]:
            dense = jnp.concatenate([dense, jnp.zeros((extent - dense.shape[0], lanes), jnp.float32)], axis=0)
        if step % 8 == 0:
            rolled = jnp.concatenate([dense[extent - step:], dense[: extent - step]], axis=0)
        else:
            rolled = pltpu.roll(dense, step, 0)
        dense = jnp.where(((start >> bit) & 1) == 1, rolled, dense)
    if dense.shape[0] < width:
        dense = jnp.concatenate([dense, jnp.zeros((width - dense.shape[0], lanes), jnp.float32)], axis=0)
    wave = jnp.dot(gt_ref[...], dense.astype(jnp.bfloat16), preferred_element_type=jnp.float32)
    rows = wave.shape[0]
    o_ref[...] = jnp.max(wave.reshape(rows // TSTEP, TSTEP, lanes), axis=1)


def wave_maxima(panel_t, coded):
    parts, height, lanes = coded.shape
    rows, width = panel_t.shape
    return pl.pallas_call(
        wave_kernel,
        grid=(parts,),
        in_specs=[
            pl.BlockSpec((rows, width), lambda p: (0, 0)),
            pl.BlockSpec((None, height, lanes), lambda p: (p, 0, 0)),
        ],
        out_specs=pl.BlockSpec((None, rows // TSTEP, lanes), lambda p: (p, 0, 0)),
        out_shape=jax.ShapeDtypeStruct((parts, rows // TSTEP, lanes), jnp.float32),
    )(panel_t, coded)


def shifted(values, step, fill):
    pad = jnp.full((abs(step),) + values.shape[1:], fill, values.dtype)
    if step > 0:
        return jnp.concatenate([pad, values[:-step]], axis=0)
    return jnp.concatenate([values[-step:], pad], axis=0)


def run_max(values, codes, reach, sign):
    step = 1
    while step < reach:
        other = shifted(values, sign * step, -jnp.inf)
        same = shifted(codes, sign * step, 0.0) == codes
        values = jnp.where(same, jnp.maximum(values, other), values)
        step *= 2
    return values


def point_peaks(window_max_t, win_point, reach):
    windows, scen = window_max_t.shape
    codes = (win_point + 1).astype(jnp.float32)[:, None]
    forward = run_max(window_max_t, codes, reach, 1)
    backward = run_max(window_max_t, codes, reach, -1)
    peak = jnp.maximum(forward, backward)
    count = lax.axis_size("rows")
    to_right = jnp.concatenate([forward[windows - 1:], jnp.broadcast_to(codes[windows - 1:], (1, scen))], axis=0)
    to_left = jnp.concatenate([backward[:1], jnp.broadcast_to(codes[:1], (1, scen))], axis=0)
    from_left = lax.ppermute(to_right, "rows", [(i, i + 1) for i in range(count - 1)])
    from_right = lax.ppermute(to_left, "rows", [(i + 1, i) for i in range(count - 1)])
    peak = jnp.where(codes == from_left[1:2], jnp.maximum(peak, from_left[0:1]), peak)
    peak = jnp.where(codes == from_right[1:2], jnp.maximum(peak, from_right[0:1]), peak)
    return peak.T


def local(greens, slip_values, rupture_ids, win_point):
    parts = lax.axis_size(SPLIT)
    shares = lax.axis_size(SHARE)
    own_sources, rows = greens.shape
    width = own_sources * parts * shares
    scen = slip_values.shape[0]
    block = rows // parts

    core = lax.rem(lax.axis_index("rows"), 2)
    side = lax.axis_index(SHARE)
    half = scen // 2
    slots = slip_values.shape[1]
    listed = rupture_ids >= 0
    values = jnp.where(listed, slip_values, jnp.zeros_like(slip_values))
    starts = jnp.maximum(rupture_ids[:, 0], 0)
    values = lax.dynamic_slice_in_dim(values, core * half, half, axis=0)
    starts = lax.dynamic_slice_in_dim(starts, core * half, half)
    code = jnp.stack([starts // CODE, starts % CODE]).astype(jnp.bfloat16)
    greens_part = greens.reshape(own_sources, parts, block).transpose(1, 0, 2).reshape(parts, own_sources * block)
    slip_part = jnp.concatenate([values.reshape(-1), code.reshape(-1)])
    used = own_sources * block + slip_part.shape[0]
    message = -(-used // (16 * 128)) * (16 * 128)
    outgoing = jnp.concatenate(
        [
            greens_part,
            jnp.broadcast_to(slip_part[None], (parts, slip_part.shape[0])),
            jnp.zeros((parts, message - used), jnp.bfloat16),
        ],
        axis=1,
    ).reshape(parts, 16, message // 16)
    incoming = lax.all_to_all(outgoing, SPLIT, 0, 0, tiled=True).reshape(parts, message)
    near = incoming[:, : own_sources * block].reshape(parts, own_sources, block)
    got = incoming[:, own_sources * block: used]
    got_values = got[:, : half * slots].reshape(parts, half, slots).transpose(0, 2, 1)
    got_code = got[:, half * slots:].reshape(parts, 2, half)
    mine = jnp.concatenate([got_values, got_code, jnp.zeros((parts, 14, half), jnp.bfloat16)], axis=1)
    count_rows = lax.axis_size("rows")
    far = lax.ppermute(near, SHARE, [(i, (i + 1) % shares) for i in range(shares)])
    theirs = lax.ppermute(mine, "rows", [(i, i ^ 1) for i in range(count_rows)])
    coded = jnp.where(core == 0, jnp.concatenate([mine, theirs], axis=2), jnp.concatenate([theirs, mine], axis=2))
    panel = jnp.where(side == 0, jnp.stack([near, far], axis=1), jnp.stack([far, near], axis=1))
    panel_t = panel.reshape(width, block).T

    maxima = wave_maxima(panel_t, coded)
    maxima = lax.all_to_all(maxima, SPLIT, 0, 0, tiled=True)
    return point_peaks(maxima.reshape(-1, scen), win_point, MOST)


def solution(mesh):
    split = Mesh(mesh.devices.reshape(mesh.shape["rows"], 8, 2), ("rows", "cols_0", "cols_1"))
    in_specs = (P(COLS, "rows"), P(COLS, None), P(COLS, None), P("rows"))
    out_specs = P(COLS, "rows")
    return jax.shard_map(local, mesh=split, in_specs=in_specs, out_specs=out_specs, check_vma=False)
```

```python
import jax
import jax.numpy as jnp
from jax import lax
from jax.experimental import pallas as pl
from jax.experimental.pallas import tpu as pltpu
from jax.sharding import Mesh
from jax.sharding import PartitionSpec as P

TSTEP = 64
COLS = ("cols_0", "cols_1")
SPLIT = "cols_0"
SHARE = "cols_1"
CODE = 32
MOST = 32


def wave_kernel(gt_ref, a_ref, o_ref):
    slots = a_ref.shape[0] - 16
    width = gt_ref.shape[1]
    lanes = a_ref.shape[1]
    code = a_ref[slots:slots + 16, :].astype(jnp.float32)
    start = (code[0:1] * CODE + code[1:2]).astype(jnp.int32)
    dense = a_ref[0:slots, :].astype(jnp.float32)
    reach = slots
    for bit in range(max(1, (width - 1).bit_length())):
        step = 1 << bit
        reach = reach + step
        extent = min(width, -(-reach // 8) * 8)
        if extent > dense.shape[0]:
            dense = jnp.concatenate([dense, jnp.zeros((extent - dense.shape[0], lanes), jnp.float32)], axis=0)
        if step % 8 == 0:
            rolled = jnp.concatenate([dense[extent - step:], dense[: extent - step]], axis=0)
        else:
            rolled = pltpu.roll(dense, step, 0)
        dense = jnp.where(((start >> bit) & 1) == 1, rolled, dense)
    if dense.shape[0] < width:
        dense = jnp.concatenate([dense, jnp.zeros((width - dense.shape[0], lanes), jnp.float32)], axis=0)
    wave = jnp.dot(gt_ref[...], dense.astype(jnp.bfloat16), preferred_element_type=jnp.float32)
    rows = wave.shape[0]
    o_ref[...] = jnp.max(wave.reshape(rows // TSTEP, TSTEP, lanes), axis=1)


def wave_maxima(panel_t, coded):
    parts, height, lanes = coded.shape
    rows, width = panel_t.shape
    return pl.pallas_call(
        wave_kernel,
        grid=(parts,),
        in_specs=[
            pl.BlockSpec((rows, width), lambda p: (0, 0)),
            pl.BlockSpec((None, height, lanes), lambda p: (p, 0, 0)),
        ],
        out_specs=pl.BlockSpec((None, rows // TSTEP, lanes), lambda p: (p, 0, 0)),
        out_shape=jax.ShapeDtypeStruct((parts, rows // TSTEP, lanes), jnp.float32),
    )(panel_t, coded)


def shifted(values, step, fill):
    pad = jnp.full((abs(step),) + values.shape[1:], fill, values.dtype)
    if step > 0:
        return jnp.concatenate([pad, values[:-step]], axis=0)
    return jnp.concatenate([values[-step:], pad], axis=0)


def run_max(values, codes, reach, sign):
    step = 1
    while step < reach:
        other = shifted(values, sign * step, -jnp.inf)
        same = shifted(codes, sign * step, 0.0) == codes
        values = jnp.where(same, jnp.maximum(values, other), values)
        step *= 2
    return values


def point_peaks(window_max_t, win_point, reach):
    windows, scen = window_max_t.shape
    codes = (win_point + 1).astype(jnp.float32)[:, None]
    forward = run_max(window_max_t, codes, reach, 1)
    backward = run_max(window_max_t, codes, reach, -1)
    peak = jnp.maximum(forward, backward)
    count = lax.axis_size("rows")
    to_right = jnp.concatenate([forward[windows - 1:], jnp.broadcast_to(codes[windows - 1:], (1, scen))], axis=0)
    to_left = jnp.concatenate([backward[:1], jnp.broadcast_to(codes[:1], (1, scen))], axis=0)
    from_left = lax.ppermute(to_right, "rows", [(i, i + 1) for i in range(count - 1)])
    from_right = lax.ppermute(to_left, "rows", [(i + 1, i) for i in range(count - 1)])
    peak = jnp.where(codes == from_left[1:2], jnp.maximum(peak, from_left[0:1]), peak)
    peak = jnp.where(codes == from_right[1:2], jnp.maximum(peak, from_right[0:1]), peak)
    return peak.T


def local(greens, slip_values, rupture_ids, win_point):
    parts = lax.axis_size(SPLIT)
    shares = lax.axis_size(SHARE)
    own_sources, rows = greens.shape
    width = own_sources * parts * shares
    scen = slip_values.shape[0]
    block = rows // parts

    listed = rupture_ids >= 0
    values = jnp.where(listed, slip_values, jnp.zeros_like(slip_values))
    starts = jnp.maximum(rupture_ids[:, 0], 0)
    code = jnp.stack([starts // CODE, starts % CODE]).astype(jnp.bfloat16)
    coded = jnp.concatenate([values.T, code], axis=0)
    core = lax.rem(lax.axis_index("rows"), 2)
    side = lax.axis_index(SHARE)
    half = scen // 2
    mine = lax.dynamic_slice_in_dim(coded, core * half, half, axis=1)
    height = mine.shape[0]
    greens_part = greens.reshape(own_sources, parts, block).transpose(1, 0, 2).reshape(parts, own_sources * block)
    slips_part = jnp.broadcast_to(mine.reshape(1, height * half), (parts, height * half))
    used = own_sources * block + height * half
    message = -(-used // (16 * 128)) * (16 * 128)
    outgoing = jnp.concatenate(
        [greens_part, slips_part, jnp.zeros((parts, message - used), jnp.bfloat16)], axis=1
    ).reshape(parts, 16, message // 16)
    incoming = lax.all_to_all(outgoing, SPLIT, 0, 0, tiled=True).reshape(parts, message)
    near = incoming[:, : own_sources * block].reshape(parts, own_sources, block)
    mine = incoming[:, own_sources * block: used].reshape(parts, height, half)
    count_rows = lax.axis_size("rows")
    far = lax.ppermute(near, SHARE, [(i, (i + 1) % shares) for i in range(shares)])
    theirs = lax.ppermute(mine, "rows", [(i, i ^ 1) for i in range(count_rows)])
    coded = jnp.where(core == 0, jnp.concatenate([mine, theirs], axis=2), jnp.concatenate([theirs, mine], axis=2))
    coded = jnp.pad(coded, ((0, 0), (0, 16 - (height - slip_values.shape[1])), (0, 0)))
    panel = jnp.where(side == 0, jnp.stack([near, far], axis=1), jnp.stack([far, near], axis=1))
    panel_t = panel.reshape(width, block).T

    maxima = wave_maxima(panel_t, coded)
    maxima = lax.all_to_all(maxima, SPLIT, 0, 0, tiled=True)
    return point_peaks(maxima.reshape(-1, scen), win_point, MOST)


def solution(mesh):
    split = Mesh(mesh.devices.reshape(mesh.shape["rows"], 8, 2), ("rows", "cols_0", "cols_1"))
    in_specs = (P(COLS, "rows"), P(COLS, None), P(COLS, None), P("rows"))
    out_specs = P(COLS, "rows")
    return jax.shard_map(local, mesh=split, in_specs=in_specs, out_specs=out_specs, check_vma=False)
```

```python
import jax
import jax.numpy as jnp
from jax import lax
from jax.experimental import pallas as pl
from jax.experimental.pallas import tpu as pltpu
from jax.sharding import Mesh
from jax.sharding import PartitionSpec as P

TSTEP = 64
COLS = ("cols_0", "cols_1")
SPLIT = "cols_0"
SHARE = "cols_1"
CODE = 32
MOST = 32


def wave_kernel(gt_ref, a_ref, o_ref):
    slots = a_ref.shape[0] - 16
    width = gt_ref.shape[0]
    lanes = a_ref.shape[1]
    code = a_ref[slots:slots + 16, :].astype(jnp.float32)
    start = (code[0:1] * CODE + code[1:2]).astype(jnp.int32)
    dense = a_ref[0:slots, :].astype(jnp.float32)
    reach = slots
    for bit in range(max(1, (width - 1).bit_length())):
        step = 1 << bit
        reach = reach + step
        extent = min(width, -(-reach // 8) * 8)
        if extent > dense.shape[0]:
            dense = jnp.concatenate([dense, jnp.zeros((extent - dense.shape[0], lanes), jnp.float32)], axis=0)
        if step % 8 == 0:
            rolled = jnp.concatenate([dense[extent - step:], dense[: extent - step]], axis=0)
        else:
            rolled = pltpu.roll(dense, step, 0)
        dense = jnp.where(((start >> bit) & 1) == 1, rolled, dense)
    if dense.shape[0] < width:
        dense = jnp.concatenate([dense, jnp.zeros((width - dense.shape[0], lanes), jnp.float32)], axis=0)
    wave = lax.dot_general(
        gt_ref[...], dense.astype(jnp.bfloat16), (((0,), (0,)), ((), ())), preferred_element_type=jnp.float32
    )
    rows = wave.shape[0]
    o_ref[...] = jnp.max(wave.reshape(rows // TSTEP, TSTEP, lanes), axis=1)


def wave_maxima(panel, coded):
    parts, height, lanes = coded.shape
    width, rows = panel.shape
    return pl.pallas_call(
        wave_kernel,
        grid=(parts,),
        in_specs=[
            pl.BlockSpec((width, rows), lambda p: (0, 0)),
            pl.BlockSpec((None, height, lanes), lambda p: (p, 0, 0)),
        ],
        out_specs=pl.BlockSpec((None, rows // TSTEP, lanes), lambda p: (p, 0, 0)),
        out_shape=jax.ShapeDtypeStruct((parts, rows // TSTEP, lanes), jnp.float32),
    )(panel, coded)


def shifted(values, step, fill):
    pad = jnp.full((abs(step),) + values.shape[1:], fill, values.dtype)
    if step > 0:
        return jnp.concatenate([pad, values[:-step]], axis=0)
    return jnp.concatenate([values[-step:], pad], axis=0)


def run_max(values, codes, reach, sign):
    step = 1
    while step < reach:
        other = shifted(values, sign * step, -jnp.inf)
        same = shifted(codes, sign * step, 0.0) == codes
        values = jnp.where(same, jnp.maximum(values, other), values)
        step *= 2
    return values


def point_peaks(window_max_t, win_point, reach):
    windows, scen = window_max_t.shape
    codes = (win_point + 1).astype(jnp.float32)[:, None]
    forward = run_max(window_max_t, codes, reach, 1)
    backward = run_max(window_max_t, codes, reach, -1)
    peak = jnp.maximum(forward, backward)
    count = lax.axis_size("rows")
    to_right = jnp.concatenate([forward[windows - 1:], jnp.broadcast_to(codes[windows - 1:], (1, scen))], axis=0)
    to_left = jnp.concatenate([backward[:1], jnp.broadcast_to(codes[:1], (1, scen))], axis=0)
    from_left = lax.ppermute(to_right, "rows", [(i, i + 1) for i in range(count - 1)])
    from_right = lax.ppermute(to_left, "rows", [(i + 1, i) for i in range(count - 1)])
    peak = jnp.where(codes == from_left[1:2], jnp.maximum(peak, from_left[0:1]), peak)
    peak = jnp.where(codes == from_right[1:2], jnp.maximum(peak, from_right[0:1]), peak)
    return peak.T


def local(greens, slip_values, rupture_ids, win_point):
    parts = lax.axis_size(SPLIT)
    shares = lax.axis_size(SHARE)
    own_sources, rows = greens.shape
    width = own_sources * parts * shares
    scen = slip_values.shape[0]
    block = rows // parts

    listed = rupture_ids >= 0
    values = jnp.where(listed, slip_values, jnp.zeros_like(slip_values))
    starts = jnp.maximum(rupture_ids[:, 0], 0)
    code = jnp.stack([starts // CODE, starts % CODE]).astype(jnp.bfloat16)
    coded = jnp.concatenate([values.T, code], axis=0)
    core = lax.rem(lax.axis_index("rows"), 2)
    side = lax.axis_index(SHARE)
    half = scen // 2
    mine = lax.dynamic_slice_in_dim(coded, core * half, half, axis=1)
    height = mine.shape[0]
    greens_part = greens.reshape(own_sources, parts, block).transpose(1, 0, 2).reshape(parts, own_sources * block)
    slips_part = jnp.broadcast_to(mine.reshape(1, height * half), (parts, height * half))
    used = own_sources * block + height * half
    message = -(-used // (16 * 128)) * (16 * 128)
    outgoing = jnp.concatenate(
        [greens_part, slips_part, jnp.zeros((parts, message - used), jnp.bfloat16)], axis=1
    ).reshape(parts, 16, message // 16)
    incoming = lax.all_to_all(outgoing, SPLIT, 0, 0, tiled=True).reshape(parts, message)
    near = incoming[:, : own_sources * block].reshape(parts, own_sources, block)
    mine = incoming[:, own_sources * block: used].reshape(parts, height, half)
    count_rows = lax.axis_size("rows")
    far = lax.ppermute(near, SHARE, [(i, (i + 1) % shares) for i in range(shares)])
    theirs = lax.ppermute(mine, "rows", [(i, i ^ 1) for i in range(count_rows)])
    coded = jnp.where(core == 0, jnp.concatenate([mine, theirs], axis=2), jnp.concatenate([theirs, mine], axis=2))
    coded = jnp.pad(coded, ((0, 0), (0, 16 - (height - slip_values.shape[1])), (0, 0)))
    panel = jnp.where(side == 0, jnp.stack([near, far], axis=1), jnp.stack([far, near], axis=1))
    maxima = wave_maxima(panel.reshape(width, block), coded)
    maxima = lax.all_to_all(maxima, SPLIT, 0, 0, tiled=True)
    return point_peaks(maxima.reshape(-1, scen), win_point, MOST)


def solution(mesh):
    split = Mesh(mesh.devices.reshape(mesh.shape["rows"], 8, 2), ("rows", "cols_0", "cols_1"))
    in_specs = (P(COLS, "rows"), P(COLS, None), P(COLS, None), P("rows"))
    out_specs = P(COLS, "rows")
    return jax.shard_map(local, mesh=split, in_specs=in_specs, out_specs=out_specs, check_vma=False)
```

```python
import jax
import jax.numpy as jnp
from jax import lax
from jax.experimental import pallas as pl
from jax.experimental.pallas import tpu as pltpu
from jax.sharding import Mesh
from jax.sharding import PartitionSpec as P

TSTEP = 64
COLS = ("cols_0", "cols_1")
SPLIT = "cols_0"
SHARE = "cols_1"
CODE = 32
MOST = 32


def wave_kernel(gt_ref, a_ref, o_ref):
    slots = a_ref.shape[0] - 2
    width = gt_ref.shape[1]
    lanes = a_ref.shape[1]
    code = a_ref[slots:slots + 2, :].astype(jnp.float32)
    start = (code[0:1] * CODE + code[1:2]).astype(jnp.int32)
    dense = a_ref[0:slots, :].astype(jnp.float32)
    reach = slots
    for bit in range(max(1, (width - 1).bit_length())):
        step = 1 << bit
        reach = reach + step
        extent = min(width, -(-reach // 8) * 8)
        if extent > dense.shape[0]:
            dense = jnp.concatenate([dense, jnp.zeros((extent - dense.shape[0], lanes), jnp.float32)], axis=0)
        if step % 8 == 0:
            rolled = jnp.concatenate([dense[extent - step:], dense[: extent - step]], axis=0)
        else:
            rolled = pltpu.roll(dense, step, 0)
        dense = jnp.where(((start >> bit) & 1) == 1, rolled, dense)
    if dense.shape[0] < width:
        dense = jnp.concatenate([dense, jnp.zeros((width - dense.shape[0], lanes), jnp.float32)], axis=0)
    wave = jnp.dot(gt_ref[...], dense.astype(jnp.bfloat16), preferred_element_type=jnp.float32)
    rows = wave.shape[0]
    o_ref[...] = jnp.max(wave.reshape(rows // TSTEP, TSTEP, lanes), axis=1)


def wave_maxima(panel_t, coded):
    parts, height, lanes = coded.shape
    rows, width = panel_t.shape
    return pl.pallas_call(
        wave_kernel,
        grid=(parts,),
        in_specs=[
            pl.BlockSpec((rows, width), lambda p: (0, 0)),
            pl.BlockSpec((None, height, lanes), lambda p: (p, 0, 0)),
        ],
        out_specs=pl.BlockSpec((None, rows // TSTEP, lanes), lambda p: (p, 0, 0)),
        out_shape=jax.ShapeDtypeStruct((parts, rows // TSTEP, lanes), jnp.float32),
    )(panel_t, coded)


def shifted(values, step, fill):
    pad = jnp.full((abs(step),) + values.shape[1:], fill, values.dtype)
    if step > 0:
        return jnp.concatenate([pad, values[:-step]], axis=0)
    return jnp.concatenate([values[-step:], pad], axis=0)


def run_max(values, codes, reach, sign):
    step = 1
    while step < reach:
        other = shifted(values, sign * step, -jnp.inf)
        same = shifted(codes, sign * step, 0.0) == codes
        values = jnp.where(same, jnp.maximum(values, other), values)
        step *= 2
    return values


def point_peaks(window_max_t, win_point, reach):
    windows, scen = window_max_t.shape
    codes = (win_point + 1).astype(jnp.float32)[:, None]
    forward = run_max(window_max_t, codes, reach, 1)
    backward = run_max(window_max_t, codes, reach, -1)
    peak = jnp.maximum(forward, backward)
    count = lax.axis_size("rows")
    to_right = jnp.concatenate([forward[windows - 1:], jnp.broadcast_to(codes[windows - 1:], (1, scen))], axis=0)
    to_left = jnp.concatenate([backward[:1], jnp.broadcast_to(codes[:1], (1, scen))], axis=0)
    from_left = lax.ppermute(to_right, "rows", [(i, i + 1) for i in range(count - 1)])
    from_right = lax.ppermute(to_left, "rows", [(i + 1, i) for i in range(count - 1)])
    peak = jnp.where(codes == from_left[1:2], jnp.maximum(peak, from_left[0:1]), peak)
    peak = jnp.where(codes == from_right[1:2], jnp.maximum(peak, from_right[0:1]), peak)
    return peak.T


def local(greens, slip_values, rupture_ids, win_point):
    parts = lax.axis_size(SPLIT)
    shares = lax.axis_size(SHARE)
    own_sources, rows = greens.shape
    width = own_sources * parts * shares
    scen = slip_values.shape[0]
    block = rows // parts

    listed = rupture_ids >= 0
    values = jnp.where(listed, slip_values, jnp.zeros_like(slip_values))
    starts = jnp.maximum(rupture_ids[:, 0], 0)
    code = jnp.stack([starts // CODE, starts % CODE]).astype(jnp.bfloat16)
    coded = jnp.concatenate([values.T, code], axis=0)
    core = lax.rem(lax.axis_index("rows"), 2)
    side = lax.axis_index(SHARE)
    half = scen // 2
    mine = lax.dynamic_slice_in_dim(coded, core * half, half, axis=1)
    height = mine.shape[0]
    greens_part = greens.reshape(own_sources, parts, block).transpose(1, 0, 2).reshape(parts, own_sources * block)
    slips_part = jnp.broadcast_to(mine.reshape(1, height * half), (parts, height * half))
    used = own_sources * block + height * half
    message = -(-used // (16 * 128)) * (16 * 128)
    outgoing = jnp.concatenate(
        [greens_part, slips_part, jnp.zeros((parts, message - used), jnp.bfloat16)], axis=1
    ).reshape(parts, 16, message // 16)
    incoming = lax.all_to_all(outgoing, SPLIT, 0, 0, tiled=True).reshape(parts, message)
    near = incoming[:, : own_sources * block].reshape(parts, own_sources, block)
    mine = incoming[:, own_sources * block: used].reshape(parts, height, half)
    count_rows = lax.axis_size("rows")
    far = lax.ppermute(near, SHARE, [(i, (i + 1) % shares) for i in range(shares)])
    theirs = lax.ppermute(mine, "rows", [(i, i ^ 1) for i in range(count_rows)])
    coded = jnp.where(core == 0, jnp.concatenate([mine, theirs], axis=2), jnp.concatenate([theirs, mine], axis=2))
    panel = jnp.where(side == 0, jnp.stack([near, far], axis=1), jnp.stack([far, near], axis=1))
    panel_t = panel.reshape(width, block).T

    maxima = wave_maxima(panel_t, coded)
    maxima = lax.all_to_all(maxima, SPLIT, 0, 0, tiled=True)
    return point_peaks(maxima.reshape(-1, scen), win_point, MOST)


def solution(mesh):
    split = Mesh(mesh.devices.reshape(mesh.shape["rows"], 8, 2), ("rows", "cols_0", "cols_1"))
    in_specs = (P(COLS, "rows"), P(COLS, None), P(COLS, None), P("rows"))
    out_specs = P(COLS, "rows")
    return jax.shard_map(local, mesh=split, in_specs=in_specs, out_specs=out_specs, check_vma=False)
```

```python
import jax
import jax.numpy as jnp
from jax import lax
from jax.experimental import pallas as pl
from jax.experimental.pallas import tpu as pltpu
from jax.sharding import Mesh
from jax.sharding import PartitionSpec as P

TSTEP = 64
COLS = ("cols_0", "cols_1")
SPLIT = "cols_0"
SHARE = "cols_1"
CODE = 32
MOST = 32


def wave_kernel(gt_ref, a_ref, o_ref):
    slots = a_ref.shape[0] - 2
    width = gt_ref.shape[0]
    lanes = a_ref.shape[1]
    code = a_ref[slots:slots + 2, :].astype(jnp.float32)
    start = (code[0:1] * CODE + code[1:2]).astype(jnp.int32)
    dense = a_ref[0:slots, :].astype(jnp.float32)
    reach = slots
    for bit in range(max(1, (width - 1).bit_length())):
        step = 1 << bit
        reach = reach + step
        extent = min(width, -(-reach // 8) * 8)
        if extent > dense.shape[0]:
            dense = jnp.concatenate([dense, jnp.zeros((extent - dense.shape[0], lanes), jnp.float32)], axis=0)
        if step % 8 == 0:
            rolled = jnp.concatenate([dense[extent - step:], dense[: extent - step]], axis=0)
        else:
            rolled = pltpu.roll(dense, step, 0)
        dense = jnp.where(((start >> bit) & 1) == 1, rolled, dense)
    if dense.shape[0] < width:
        dense = jnp.concatenate([dense, jnp.zeros((width - dense.shape[0], lanes), jnp.float32)], axis=0)
    wave = lax.dot_general(
        gt_ref[...], dense.astype(jnp.bfloat16), (((0,), (0,)), ((), ())), preferred_element_type=jnp.float32
    )
    rows = wave.shape[0]
    o_ref[...] = jnp.max(wave.reshape(rows // TSTEP, TSTEP, lanes), axis=1)


def wave_maxima(panel, coded):
    parts, height, lanes = coded.shape
    width, rows = panel.shape
    return pl.pallas_call(
        wave_kernel,
        grid=(parts,),
        in_specs=[
            pl.BlockSpec((width, rows), lambda p: (0, 0)),
            pl.BlockSpec((None, height, lanes), lambda p: (p, 0, 0)),
        ],
        out_specs=pl.BlockSpec((None, rows // TSTEP, lanes), lambda p: (p, 0, 0)),
        out_shape=jax.ShapeDtypeStruct((parts, rows // TSTEP, lanes), jnp.float32),
    )(panel, coded)


def shifted(values, step, fill):
    pad = jnp.full((abs(step),) + values.shape[1:], fill, values.dtype)
    if step > 0:
        return jnp.concatenate([pad, values[:-step]], axis=0)
    return jnp.concatenate([values[-step:], pad], axis=0)


def run_max(values, codes, reach, sign):
    step = 1
    while step < reach:
        other = shifted(values, sign * step, -jnp.inf)
        same = shifted(codes, sign * step, 0.0) == codes
        values = jnp.where(same, jnp.maximum(values, other), values)
        step *= 2
    return values


def point_peaks(window_max_t, win_point, reach):
    windows, scen = window_max_t.shape
    codes = (win_point + 1).astype(jnp.float32)[:, None]
    forward = run_max(window_max_t, codes, reach, 1)
    backward = run_max(window_max_t, codes, reach, -1)
    peak = jnp.maximum(forward, backward)
    count = lax.axis_size("rows")
    to_right = jnp.concatenate([forward[windows - 1:], jnp.broadcast_to(codes[windows - 1:], (1, scen))], axis=0)
    to_left = jnp.concatenate([backward[:1], jnp.broadcast_to(codes[:1], (1, scen))], axis=0)
    from_left = lax.ppermute(to_right, "rows", [(i, i + 1) for i in range(count - 1)])
    from_right = lax.ppermute(to_left, "rows", [(i + 1, i) for i in range(count - 1)])
    peak = jnp.where(codes == from_left[1:2], jnp.maximum(peak, from_left[0:1]), peak)
    peak = jnp.where(codes == from_right[1:2], jnp.maximum(peak, from_right[0:1]), peak)
    return peak.T


def local(greens, slip_values, rupture_ids, win_point):
    parts = lax.axis_size(SPLIT)
    shares = lax.axis_size(SHARE)
    own_sources, rows = greens.shape
    width = own_sources * parts * shares
    scen = slip_values.shape[0]
    block = rows // parts

    listed = rupture_ids >= 0
    values = jnp.where(listed, slip_values, jnp.zeros_like(slip_values))
    starts = jnp.maximum(rupture_ids[:, 0], 0)
    code = jnp.stack([starts // CODE, starts % CODE]).astype(jnp.bfloat16)
    coded = jnp.concatenate([values.T, code], axis=0)
    core = lax.rem(lax.axis_index("rows"), 2)
    side = lax.axis_index(SHARE)
    half = scen // 2
    mine = lax.dynamic_slice_in_dim(coded, core * half, half, axis=1)
    height = mine.shape[0]
    greens_part = greens.reshape(own_sources, parts, block).transpose(1, 0, 2).reshape(parts, own_sources * block)
    slips_part = jnp.broadcast_to(mine.reshape(1, height * half), (parts, height * half))
    used = own_sources * block + height * half
    message = -(-used // (16 * 128)) * (16 * 128)
    outgoing = jnp.concatenate(
        [greens_part, slips_part, jnp.zeros((parts, message - used), jnp.bfloat16)], axis=1
    ).reshape(parts, 16, message // 16)
    incoming = lax.all_to_all(outgoing, SPLIT, 0, 0, tiled=True).reshape(parts, message)
    near = incoming[:, : own_sources * block].reshape(parts, own_sources, block)
    mine = incoming[:, own_sources * block: used].reshape(parts, height, half)
    count_rows = lax.axis_size("rows")
    far = lax.ppermute(near, SHARE, [(i, (i + 1) % shares) for i in range(shares)])
    theirs = lax.ppermute(mine, "rows", [(i, i ^ 1) for i in range(count_rows)])
    coded = jnp.where(core == 0, jnp.concatenate([mine, theirs], axis=2), jnp.concatenate([theirs, mine], axis=2))
    panel = jnp.where(side == 0, jnp.stack([near, far], axis=1), jnp.stack([far, near], axis=1))
    maxima = wave_maxima(panel.reshape(width, block), coded)
    maxima = lax.all_to_all(maxima, SPLIT, 0, 0, tiled=True)
    return point_peaks(maxima.reshape(-1, scen), win_point, MOST)


def solution(mesh):
    split = Mesh(mesh.devices.reshape(mesh.shape["rows"], 8, 2), ("rows", "cols_0", "cols_1"))
    in_specs = (P(COLS, "rows"), P(COLS, None), P(COLS, None), P("rows"))
    out_specs = P(COLS, "rows")
    return jax.shard_map(local, mesh=split, in_specs=in_specs, out_specs=out_specs, check_vma=False)
```
